512 devices in a mesh: gx: 8 (over z_lo, core), gy: 16 (over x, z_hi), gz: 4 (over y).
Axes of the slice: x: 4, y: 4, z: 16 (z_hi: 4, z_lo: 4; z = z_hi * 4 + z_lo), core: 2. Of those that a mesh axis runs over, the one named last changes fastest.
Arguments:
- heat_source: float32 [128, 256, 512], P('gx', 'gy', 'gz'), may hold values from -6 to 6
- material: int32 [128, 256, 512], P('gx', 'gy', 'gz'), may hold values from 0 to 2
- conductivity: float32 [3], replicated, may hold values from 0.3 to 3
Outputs:
- temperature: float32 [128, 256, 512], P('gx', 'gy', 'gz')
The draws below stay inside these ranges and needn't reach their ends.
All inputs are finite; a program needn't handle non-finite values.
Results may differ from the reference program's by a relative error of at most 0.00002.
Values sent between devices are 32-bit elements; how exact they have to be, the bound alone decides.
No kernel may reach another device: no remote copies, remote signals or barrier semaphores. Data moves between devices by JAX's collectives and lax.ppermute only.
A program may use at most 192 MiB of HBM per device.

```python
import math
import jax
import jax.numpy as jnp

DEGREE = 3
LEVELS = 3
MATERIALS = 3
NX = 128
NY = 256
NZ = 512


def plant(result, rng, low, top_value):
    shape = result.shape
    place = [jax.random.randint(jax.random.fold_in(rng, axis), (), 0, shape[axis]) for axis in range(len(shape))]
    result = result.at[tuple(place)].set(low)
    longest = shape.index(max(shape))
    place[longest] = (place[longest] + 1) % shape[longest]
    return result.at[tuple(place)].set(top_value)


def levels(own_key, extent, pieces, least, largest):
    gain, own = 1.0, jax.random.fold_in(own_key, 6)
    for dim, blocks in pieces:
        steps = jnp.exp(jax.random.uniform(jax.random.fold_in(own, dim), (blocks,), jnp.float32, least / len(pieces), largest / len(pieces)))
        gain = gain * jnp.repeat(steps, extent[dim] // blocks).reshape([-1 if axis == dim else 1 for axis in range(len(extent))])
    return gain


def bell_draw(key, dims, scale, most, cuts=(), dtype=jnp.bfloat16):
    level = levels(key, dims, cuts, -0.22, 0.18) if cuts else 1.0
    entries = jax.random.normal(key, dims, jnp.float32) * scale * level
    return jnp.minimum(jnp.maximum(entries, -most), most).astype(dtype)


def setup_inputs(seed: int = 0) -> dict:
    arg_keys = jax.random.split(jax.random.key(seed), 4)
    heat_source = bell_draw(arg_keys[0], (NX, NY, NZ), 1.0, 6.0, ((0, 8), (1, 16), (2, 4)), jnp.float32)
    material = plant(jax.random.randint(arg_keys[1], (NX, NY, NZ), 0, 3), jax.random.fold_in(arg_keys[1], 1), 0, 2).astype(jnp.int32)
    conductivity = jnp.clip(jnp.exp(jax.random.uniform(arg_keys[2], (MATERIALS,), jnp.float32, math.log(0.3), math.log(3.0))), 0.3, 3.0)
    return {"heat_source": heat_source, "material": material, "conductivity": conductivity}


LOW = 0.3
HIGH = 2.0


def harmonic(left, right):
    return 2.0 * left * right / (left + right)


def neighbours(padded):
    return (padded[2:, 1:-1, 1:-1], padded[:-2, 1:-1, 1:-1], padded[1:-1, 2:, 1:-1],
            padded[1:-1, :-2, 1:-1], padded[1:-1, 1:-1, 2:], padded[1:-1, 1:-1, :-2])


def face_set(cond):
    padded = jnp.pad(cond, 1, mode="edge")
    faces = tuple(harmonic(cond, other) for other in neighbours(padded))
    diag = faces[0] + faces[1] + faces[2] + faces[3] + faces[4] + faces[5]
    return faces, diag


def operate(field, faces, diag, scale):
    near = neighbours(jnp.pad(field, 1))
    total = faces[0] * near[0] + faces[1] * near[1] + faces[2] * near[2]
    total = total + faces[3] * near[3] + faces[4] * near[4] + faces[5] * near[5]
    return scale * (diag * field - total)


def smooth(right, start, faces, diag, scale):
    theta = 0.5 * (HIGH + LOW)
    delta = 0.5 * (HIGH - LOW)
    sigma = theta / delta
    rho = 1.0 / sigma
    inverse = 1.0 / (scale * diag)
    if start is None:
        resid = right
        step_dir = inverse * resid / theta
        field = step_dir
    else:
        resid = right - operate(start, faces, diag, scale)
        step_dir = inverse * resid / theta
        field = start + step_dir
    for turn in range(DEGREE - 1):
        rho_new = 1.0 / (2.0 * sigma - rho)
        resid = right - operate(field, faces, diag, scale)
        step_dir = rho_new * rho * step_dir + (2.0 * rho_new / delta) * inverse * resid
        field = field + step_dir
        rho = rho_new
    return field


def restrict(field):
    sx, sy, sz = field.shape
    return field.reshape(sx // 2, 2, sy // 2, 2, sz // 2, 2).mean(axis=(1, 3, 5))


def prolong(field):
    return jnp.repeat(jnp.repeat(jnp.repeat(field, 2, 0), 2, 1), 2, 2)


def cycle(right, cond, level, scale):
    faces, diag = face_set(cond)
    if level == LEVELS:
        field = smooth(right, None, faces, diag, scale)
        return smooth(right, field, faces, diag, scale)
    field = smooth(right, None, faces, diag, scale)
    resid = right - operate(field, faces, diag, scale)
    error = cycle(restrict(resid), restrict(cond), level + 1, scale * 0.25)
    field = field + prolong(error)
    return smooth(right, field, faces, diag, scale)


def reference(heat_source, material, conductivity):
    cond = jnp.zeros(heat_source.shape, jnp.float32)
    for which in range(MATERIALS):
        cond = cond + jnp.where(material == which, conductivity[which], jnp.float32(0.0))
    return cycle(heat_source, cond, 0, 1.0)
```

```python
import jax
import jax.numpy as jnp
from jax import lax
from jax.sharding import PartitionSpec as P

DEGREE = 3
LEVELS = 3
MATERIALS = 3

LOW = 0.3
HIGH = 2.0

AXES = ("gx", "gy", "gz")
HALO0 = 6
HALO1 = 8


def exchange(block, width):
    for k, axis in enumerate(AXES):
        dim = block.ndim - 3 + k
        count = lax.axis_size(axis)
        forward = [(i, i + 1) for i in range(count - 1)]
        backward = [(i + 1, i) for i in range(count - 1)]
        size = block.shape[dim]
        low = lax.ppermute(lax.slice_in_dim(block, size - width, size, axis=dim), axis, forward)
        high = lax.ppermute(lax.slice_in_dim(block, 0, width, axis=dim), axis, backward)
        block = jnp.concatenate([low, block, high], axis=dim)
    return block


def inside_mask(block_shape, width):
    parts = []
    for k, axis in enumerate(AXES):
        n = block_shape[k]
        total = n * lax.axis_size(axis)
        coord = lax.axis_index(axis) * n - width + jnp.arange(n + 2 * width)
        parts.append((coord >= 0) & (coord < total))
    return parts[0][:, None, None] & parts[1][None, :, None] & parts[2][None, None, :]


def harmonic(left, right):
    return 2.0 * left * right / (left + right)


def neighbours(padded):
    return (
        padded[2:, 1:-1, 1:-1],
        padded[:-2, 1:-1, 1:-1],
        padded[1:-1, 2:, 1:-1],
        padded[1:-1, :-2, 1:-1],
        padded[1:-1, 1:-1, 2:],
        padded[1:-1, 1:-1, :-2],
    )


def face_set_zero_outside(cond):
    padded = jnp.pad(cond, 1)
    faces = tuple(harmonic(cond, jnp.where(other > 0.0, other, cond)) for other in neighbours(padded))
    diag = faces[0] + faces[1] + faces[2] + faces[3] + faces[4] + faces[5]
    return faces, diag


def face_set_global(cond):
    padded = jnp.pad(cond, 1, mode="edge")
    faces = tuple(harmonic(cond, other) for other in neighbours(padded))
    diag = faces[0] + faces[1] + faces[2] + faces[3] + faces[4] + faces[5]
    return faces, diag


def operate(field, faces, diag, scale):
    near = neighbours(jnp.pad(field, 1))
    total = faces[0] * near[0] + faces[1] * near[1] + faces[2] * near[2]
    total = total + faces[3] * near[3] + faces[4] * near[4] + faces[5] * near[5]
    return scale * (diag * field - total)


def smooth(right, start, faces, diag, scale, mask=None):
    def keep(value):
        return value if mask is None else jnp.where(mask, value, 0.0)

    theta = 0.5 * (HIGH + LOW)
    delta = 0.5 * (HIGH - LOW)
    sigma = theta / delta
    rho = 1.0 / sigma
    inverse = 1.0 / (scale * diag)
    if start is None:
        resid = right
        step_dir = inverse * resid / theta
        field = keep(step_dir)
    else:
        resid = right - operate(start, faces, diag, scale)
        step_dir = inverse * resid / theta
        field = keep(start + step_dir)
    for turn in range(DEGREE - 1):
        rho_new = 1.0 / (2.0 * sigma - rho)
        resid = right - operate(field, faces, diag, scale)
        step_dir = rho_new * rho * step_dir + 2.0 * rho_new / delta * inverse * resid
        field = keep(field + step_dir)
        rho = rho_new
    return field


def restrict(field):
    field = field[0::2] + field[1::2]
    field = field[:, 0::2] + field[:, 1::2]
    field = field[:, :, 0::2] + field[:, :, 1::2]
    return field / 8.0


def prolong(field):
    return jnp.repeat(jnp.repeat(jnp.repeat(field, 2, 0), 2, 1), 2, 2)


def centre(field, width):
    return field[width:-width, width:-width, width:-width]


def cycle_global(right, cond, level, scale):
    faces, diag = face_set_global(cond)
    if level == LEVELS:
        field = smooth(right, None, faces, diag, scale)
        return smooth(right, field, faces, diag, scale)
    field = smooth(right, None, faces, diag, scale)
    resid = right - operate(field, faces, diag, scale)
    error = cycle_global(restrict(resid), restrict(cond), level + 1, scale * 0.25)
    field = field + prolong(error)
    return smooth(right, field, faces, diag, scale)


def gather_global(block):
    sizes = [lax.axis_size(axis) for axis in AXES]
    c, bx, by, bz = block.shape
    every = lax.all_gather(block, AXES, axis=0, tiled=False)
    every = every.reshape(sizes[0], sizes[1], sizes[2], c, bx, by, bz)
    every = every.transpose(3, 0, 4, 1, 5, 2, 6)
    return every.reshape(c, sizes[0] * bx, sizes[1] * by, sizes[2] * bz)


def local(heat_source, material, conductivity):
    cond0 = jnp.zeros(heat_source.shape, jnp.float32)
    for which in range(MATERIALS):
        cond0 = cond0 + jnp.where(material == which, conductivity[which], jnp.float32(0.0))
    cond1 = restrict(cond0)
    cond2 = restrict(cond1)
    block0, block1 = heat_source.shape, cond1.shape

    ext0 = exchange(jnp.stack([cond0, heat_source]), HALO0)
    cond0e, right0e = ext0[0], ext0[1]
    mask0 = inside_mask(block0, HALO0)
    faces0, diag0 = face_set_zero_outside(cond0e)
    field0 = smooth(right0e, None, faces0, diag0, 1.0, mask0)
    resid0 = centre(right0e - operate(field0, faces0, diag0, 1.0), HALO0)

    cond1e = exchange(cond1, HALO1)
    faces1, diag1 = face_set_zero_outside(cond1e)
    mask1 = inside_mask(block1, HALO1)
    right1e = exchange(restrict(resid0), HALO1)
    field1 = smooth(right1e, None, faces1, diag1, 0.25, mask1)
    resid1 = centre(right1e - operate(field1, faces1, diag1, 0.25), HALO1)

    whole = gather_global(jnp.stack([cond2, restrict(resid1)]))
    error2 = cycle_global(whole[1], whole[0], 2, 0.0625)

    reach = HALO1 // 2
    padded2 = jnp.pad(error2, reach)
    block2 = cond2.shape
    starts = [lax.axis_index(axis) * n for axis, n in zip(AXES, block2)]
    sizes = [n + 2 * reach for n in block2]
    error2e = lax.dynamic_slice(padded2, starts, sizes)
    field1 = jnp.where(mask1, field1 + prolong(error2e), 0.0)
    field1 = smooth(right1e, field1, faces1, diag1, 0.25, mask1)

    cut = HALO1 - HALO0 // 2
    error1e = field1[cut:-cut, cut:-cut, cut:-cut]
    field0 = jnp.where(mask0, field0 + prolong(error1e), 0.0)
    field0 = smooth(right0e, field0, faces0, diag0, 1.0, mask0)
    return centre(field0, HALO0)


def solution(mesh):
    in_specs = (P("gx", "gy", "gz"), P("gx", "gy", "gz"), P())
    out_specs = P("gx", "gy", "gz")
    return jax.shard_map(local, mesh=mesh, in_specs=in_specs, out_specs=out_specs, check_vma=False)
```

```python
import jax
import jax.numpy as jnp
from jax import lax
from jax.sharding import PartitionSpec as P

DEGREE = 3
LEVELS = 3
MATERIALS = 3

LOW = 0.3
HIGH = 2.0

AXES = ("gx", "gy", "gz")
HALO0 = 6
HALO1 = 8


def exchange(block, width):
    for k, axis in enumerate(AXES):
        dim = block.ndim - 3 + k
        count = lax.axis_size(axis)
        forward = [(i, i + 1) for i in range(count - 1)]
        backward = [(i + 1, i) for i in range(count - 1)]
        size = block.shape[dim]
        low = lax.ppermute(lax.slice_in_dim(block, size - width, size, axis=dim), axis, forward)
        high = lax.ppermute(lax.slice_in_dim(block, 0, width, axis=dim), axis, backward)
        block = jnp.concatenate([low, block, high], axis=dim)
    return block


def inside_mask(block_shape, width):
    parts = []
    for k, axis in enumerate(AXES):
        n = block_shape[k]
        total = n * lax.axis_size(axis)
        coord = lax.axis_index(axis) * n - width + jnp.arange(n + 2 * width)
        parts.append((coord >= 0) & (coord < total))
    return parts[0][:, None, None] & parts[1][None, :, None] & parts[2][None, None, :]


def harmonic(left, right):
    return 2.0 * left * right / (left + right)


def neighbours(padded):
    return (
        padded[2:, 1:-1, 1:-1],
        padded[:-2, 1:-1, 1:-1],
        padded[1:-1, 2:, 1:-1],
        padded[1:-1, :-2, 1:-1],
        padded[1:-1, 1:-1, 2:],
        padded[1:-1, 1:-1, :-2],
    )


def face_set_zero_outside(cond):
    padded = jnp.pad(cond, 1)
    faces = tuple(harmonic(cond, jnp.where(other > 0.0, other, cond)) for other in neighbours(padded))
    diag = faces[0] + faces[1] + faces[2] + faces[3] + faces[4] + faces[5]
    return faces, diag


def operate(field, faces, diag, scale):
    near = neighbours(jnp.pad(field, 1))
    total = faces[0] * near[0] + faces[1] * near[1] + faces[2] * near[2]
    total = total + faces[3] * near[3] + faces[4] * near[4] + faces[5] * near[5]
    return scale * (diag * field - total)


def smooth(right, start, faces, diag, scale, mask=None):
    def keep(value):
        return value if mask is None else jnp.where(mask, value, 0.0)

    theta = 0.5 * (HIGH + LOW)
    delta = 0.5 * (HIGH - LOW)
    sigma = theta / delta
    rho = 1.0 / sigma
    inverse = 1.0 / (scale * diag)
    if start is None:
        resid = right
        step_dir = inverse * resid / theta
        field = keep(step_dir)
    else:
        resid = right - operate(start, faces, diag, scale)
        step_dir = inverse * resid / theta
        field = keep(start + step_dir)
    for turn in range(DEGREE - 1):
        rho_new = 1.0 / (2.0 * sigma - rho)
        resid = right - operate(field, faces, diag, scale)
        step_dir = rho_new * rho * step_dir + 2.0 * rho_new / delta * inverse * resid
        field = keep(field + step_dir)
        rho = rho_new
    return field


def restrict(field):
    field = field[0::2] + field[1::2]
    field = field[:, 0::2] + field[:, 1::2]
    field = field[:, :, 0::2] + field[:, :, 1::2]
    return field / 8.0


def prolong(field):
    return jnp.repeat(jnp.repeat(jnp.repeat(field, 2, 0), 2, 1), 2, 2)


def centre(field, width):
    return field[width:-width, width:-width, width:-width]


def exchange_faces(block):
    padded = jnp.pad(block, 1)
    inner = [slice(1, -1)] * 3
    for k, axis in enumerate(AXES):
        count = lax.axis_size(axis)
        forward = [(i, i + 1) for i in range(count - 1)]
        backward = [(i + 1, i) for i in range(count - 1)]
        size = block.shape[k]
        low = lax.ppermute(lax.slice_in_dim(block, size - 1, size, axis=k), axis, forward)
        high = lax.ppermute(lax.slice_in_dim(block, 0, 1, axis=k), axis, backward)
        at_low = list(inner)
        at_low[k] = slice(0, 1)
        at_high = list(inner)
        at_high[k] = slice(size + 1, size + 2)
        padded = padded.at[tuple(at_low)].set(low).at[tuple(at_high)].set(high)
    return padded


def face_set_faces(cond):
    padded = exchange_faces(cond)
    faces = tuple(harmonic(cond, jnp.where(other > 0.0, other, cond)) for other in neighbours(padded))
    diag = faces[0] + faces[1] + faces[2] + faces[3] + faces[4] + faces[5]
    return faces, diag


def operate_faces(field, faces, diag, scale):
    near = neighbours(exchange_faces(field))
    total = faces[0] * near[0] + faces[1] * near[1] + faces[2] * near[2]
    total = total + faces[3] * near[3] + faces[4] * near[4] + faces[5] * near[5]
    return scale * (diag * field - total)


def smooth_faces(right, start, faces, diag, scale):
    theta = 0.5 * (HIGH + LOW)
    delta = 0.5 * (HIGH - LOW)
    sigma = theta / delta
    rho = 1.0 / sigma
    inverse = 1.0 / (scale * diag)
    if start is None:
        resid = right
        step_dir = inverse * resid / theta
        field = step_dir
    else:
        resid = right - operate_faces(start, faces, diag, scale)
        step_dir = inverse * resid / theta
        field = start + step_dir
    for turn in range(DEGREE - 1):
        rho_new = 1.0 / (2.0 * sigma - rho)
        resid = right - operate_faces(field, faces, diag, scale)
        step_dir = rho_new * rho * step_dir + 2.0 * rho_new / delta * inverse * resid
        field = field + step_dir
        rho = rho_new
    return field


def cycle_faces(right, cond, level, scale):
    faces, diag = face_set_faces(cond)
    if level == LEVELS:
        field = smooth_faces(right, None, faces, diag, scale)
        return smooth_faces(right, field, faces, diag, scale)
    field = smooth_faces(right, None, faces, diag, scale)
    resid = right - operate_faces(field, faces, diag, scale)
    error = cycle_faces(restrict(resid), restrict(cond), level + 1, scale * 0.25)
    field = field + prolong(error)
    return smooth_faces(right, field, faces, diag, scale)


def local(heat_source, material, conductivity):
    cond0 = jnp.zeros(heat_source.shape, jnp.float32)
    for which in range(MATERIALS):
        cond0 = cond0 + jnp.where(material == which, conductivity[which], jnp.float32(0.0))
    cond1 = restrict(cond0)
    cond2 = restrict(cond1)
    block0, block1 = heat_source.shape, cond1.shape

    ext0 = exchange(jnp.stack([cond0, heat_source]), HALO0)
    cond0e, right0e = ext0[0], ext0[1]
    mask0 = inside_mask(block0, HALO0)
    faces0, diag0 = face_set_zero_outside(cond0e)
    field0 = smooth(right0e, None, faces0, diag0, 1.0, mask0)
    resid0 = centre(right0e - operate(field0, faces0, diag0, 1.0), HALO0)

    cond1e = exchange(cond1, HALO1)
    faces1, diag1 = face_set_zero_outside(cond1e)
    mask1 = inside_mask(block1, HALO1)
    right1e = exchange(restrict(resid0), HALO1)
    field1 = smooth(right1e, None, faces1, diag1, 0.25, mask1)
    resid1 = centre(right1e - operate(field1, faces1, diag1, 0.25), HALO1)

    error2 = cycle_faces(restrict(resid1), cond2, 2, 0.0625)

    reach = HALO1 // 2
    error2e = jnp.pad(exchange(error2, 3), reach - 3)
    field1 = jnp.where(mask1, field1 + prolong(error2e), 0.0)
    field1 = smooth(right1e, field1, faces1, diag1, 0.25, mask1)

    cut = HALO1 - HALO0 // 2
    error1e = field1[cut:-cut, cut:-cut, cut:-cut]
    field0 = jnp.where(mask0, field0 + prolong(error1e), 0.0)
    field0 = smooth(right0e, field0, faces0, diag0, 1.0, mask0)
    return centre(field0, HALO0)


def solution(mesh):
    in_specs = (P("gx", "gy", "gz"), P("gx", "gy", "gz"), P())
    out_specs = P("gx", "gy", "gz")
    return jax.shard_map(local, mesh=mesh, in_specs=in_specs, out_specs=out_specs, check_vma=False)
```

```python
import jax
import jax.numpy as jnp
from jax import lax
from jax.sharding import PartitionSpec as P

DEGREE = 3
LEVELS = 3
MATERIALS = 3

LOW = 0.3
HIGH = 2.0

AXES = ("gx", "gy", "gz")
HALO0 = 6
HALO1 = 8


def exchange(block, width):
    for k, axis in enumerate(AXES):
        dim = block.ndim - 3 + k
        count = lax.axis_size(axis)
        forward = [(i, i + 1) for i in range(count - 1)]
        backward = [(i + 1, i) for i in range(count - 1)]
        size = block.shape[dim]
        low = lax.ppermute(lax.slice_in_dim(block, size - width, size, axis=dim), axis, forward)
        high = lax.ppermute(lax.slice_in_dim(block, 0, width, axis=dim), axis, backward)
        block = jnp.concatenate([low, block, high], axis=dim)
    return block


def inside_mask(block_shape, width):
    parts = []
    for k, axis in enumerate(AXES):
        n = block_shape[k]
        total = n * lax.axis_size(axis)
        coord = lax.axis_index(axis) * n - width + jnp.arange(n + 2 * width)
        parts.append((coord >= 0) & (coord < total))
    return parts[0][:, None, None] & parts[1][None, :, None] & parts[2][None, None, :]


def harmonic(left, right):
    return 2.0 * left * right / (left + right)


def neighbours(padded):
    return (
        padded[2:, 1:-1, 1:-1],
        padded[:-2, 1:-1, 1:-1],
        padded[1:-1, 2:, 1:-1],
        padded[1:-1, :-2, 1:-1],
        padded[1:-1, 1:-1, 2:],
        padded[1:-1, 1:-1, :-2],
    )


def face_set_zero_outside(cond):
    padded = jnp.pad(cond, 1)
    faces = tuple(harmonic(cond, jnp.where(other > 0.0, other, cond)) for other in neighbours(padded))
    diag = faces[0] + faces[1] + faces[2] + faces[3] + faces[4] + faces[5]
    return faces, diag


def operate(field, faces, diag, scale):
    near = neighbours(jnp.pad(field, 1))
    total = faces[0] * near[0] + faces[1] * near[1] + faces[2] * near[2]
    total = total + faces[3] * near[3] + faces[4] * near[4] + faces[5] * near[5]
    return scale * (diag * field - total)


def smooth(right, start, faces, diag, scale, mask=None):
    def keep(value):
        return value if mask is None else jnp.where(mask, value, 0.0)

    theta = 0.5 * (HIGH + LOW)
    delta = 0.5 * (HIGH - LOW)
    sigma = theta / delta
    rho = 1.0 / sigma
    inverse = 1.0 / (scale * diag)
    if start is None:
        resid = right
        step_dir = inverse * resid / theta
        field = keep(step_dir)
    else:
        resid = right - operate(start, faces, diag, scale)
        step_dir = inverse * resid / theta
        field = keep(start + step_dir)
    for turn in range(DEGREE - 1):
        rho_new = 1.0 / (2.0 * sigma - rho)
        resid = right - operate(field, faces, diag, scale)
        step_dir = rho_new * rho * step_dir + 2.0 * rho_new / delta * inverse * resid
        field = keep(field + step_dir)
        rho = rho_new
    return field


def restrict(field):
    field = field[0::2] + field[1::2]
    field = field[:, 0::2] + field[:, 1::2]
    field = field[:, :, 0::2] + field[:, :, 1::2]
    return field / 8.0


def prolong(field):
    return jnp.repeat(jnp.repeat(jnp.repeat(field, 2, 0), 2, 1), 2, 2)


def centre(field, width):
    return field[width:-width, width:-width, width:-width]


def face_set_global(cond):
    padded = jnp.pad(cond, 1, mode="edge")
    faces = tuple(harmonic(cond, other) for other in neighbours(padded))
    diag = faces[0] + faces[1] + faces[2] + faces[3] + faces[4] + faces[5]
    return faces, diag


def cycle_global(right, cond, level, scale):
    faces, diag = face_set_global(cond)
    if level == LEVELS:
        field = smooth(right, None, faces, diag, scale)
        return smooth(right, field, faces, diag, scale)
    field = smooth(right, None, faces, diag, scale)
    resid = right - operate(field, faces, diag, scale)
    error = cycle_global(restrict(resid), restrict(cond), level + 1, scale * 0.25)
    field = field + prolong(error)
    return smooth(right, field, faces, diag, scale)


def gather_axis(block, axis, dim):
    count = lax.axis_size(axis)
    if count & (count - 1):
        return lax.all_gather(block, axis, axis=dim, tiled=True)
    index = lax.axis_index(axis)
    step = 1
    while step < count:
        theirs = lax.ppermute(block, axis, [(i, i ^ step) for i in range(count)])
        upper = (index // step) % 2 == 1
        low = jnp.where(upper, theirs, block)
        high = jnp.where(upper, block, theirs)
        block = jnp.concatenate([low, high], axis=dim)
        step *= 2
    return block


def gather_global(block):
    block = gather_axis(block, "gz", 3)
    block = gather_axis(block, "gx", 1)
    return gather_axis(block, "gy", 2)


def local(heat_source, material, conductivity):
    cond0 = jnp.zeros(heat_source.shape, jnp.float32)
    for which in range(MATERIALS):
        cond0 = cond0 + jnp.where(material == which, conductivity[which], jnp.float32(0.0))
    cond1 = restrict(cond0)
    cond2 = restrict(cond1)
    block0, block1 = heat_source.shape, cond1.shape

    ext0 = exchange(jnp.stack([cond0, heat_source]), HALO0)
    cond0e, right0e = ext0[0], ext0[1]
    mask0 = inside_mask(block0, HALO0)
    faces0, diag0 = face_set_zero_outside(cond0e)
    field0 = smooth(right0e, None, faces0, diag0, 1.0, mask0)
    resid0 = centre(right0e - operate(field0, faces0, diag0, 1.0), HALO0)

    cond1e = exchange(cond1, HALO1)
    faces1, diag1 = face_set_zero_outside(cond1e)
    mask1 = inside_mask(block1, HALO1)
    right1e = exchange(restrict(resid0), HALO1)
    field1 = smooth(right1e, None, faces1, diag1, 0.25, mask1)
    resid1 = centre(right1e - operate(field1, faces1, diag1, 0.25), HALO1)

    whole = gather_global(jnp.stack([cond2, restrict(resid1)]))
    error2 = cycle_global(whole[1], whole[0], 2, 0.0625)

    reach = HALO1 // 2
    padded2 = jnp.pad(error2, reach)
    block2 = cond2.shape
    starts = [lax.axis_index(axis) * n for axis, n in zip(AXES, block2)]
    sizes = [n + 2 * reach for n in block2]
    error2e = lax.dynamic_slice(padded2, starts, sizes)
    field1 = jnp.where(mask1, field1 + prolong(error2e), 0.0)
    field1 = smooth(right1e, field1, faces1, diag1, 0.25, mask1)

    cut = HALO1 - HALO0 // 2
    error1e = field1[cut:-cut, cut:-cut, cut:-cut]
    field0 = jnp.where(mask0, field0 + prolong(error1e), 0.0)
    field0 = smooth(right0e, field0, faces0, diag0, 1.0, mask0)
    return centre(field0, HALO0)


def solution(mesh):
    in_specs = (P("gx", "gy", "gz"), P("gx", "gy", "gz"), P())
    out_specs = P("gx", "gy", "gz")
    return jax.shard_map(local, mesh=mesh, in_specs=in_specs, out_specs=out_specs, check_vma=False)
```

```python
import jax
import jax.numpy as jnp
from jax import lax
from jax.sharding import PartitionSpec as P

DEGREE = 3
LEVELS = 3
MATERIALS = 3

LOW = 0.3
HIGH = 2.0

AXES = ("gx", "gy", "gz")
HALO0 = 6
HALO1 = 8
HALO2 = 8


def exchange(blocks, widths):
    blocks = list(blocks)
    for k, axis in enumerate(AXES):
        count = lax.axis_size(axis)
        dims = [b.ndim - 3 + k for b in blocks]
        sizes = [b.shape[d] for b, d in zip(blocks, dims)]
        reach = [-(-w // n) for w, n in zip(widths, sizes)]
        lows = [[] for _ in blocks]
        highs = [[] for _ in blocks]
        for shift in range(1, max(reach) + 1):
            users = [j for j in range(len(blocks)) if reach[j] >= shift]
            takes = {j: min(sizes[j], widths[j] - (shift - 1) * sizes[j]) for j in users}
            for side in (0, 1):
                slabs = []
                for j in users:
                    n, t = sizes[j], takes[j]
                    start = n - t if side == 0 else 0
                    slabs.append(lax.slice_in_dim(blocks[j], start, start + t, axis=dims[j]))
                if shift >= count:
                    got = [jnp.zeros_like(s) for s in slabs]
                else:
                    if side == 0:
                        pairs = [(i, i + shift) for i in range(count - shift)]
                    else:
                        pairs = [(i + shift, i) for i in range(count - shift)]
                    flat = jnp.concatenate([s.reshape(-1) for s in slabs])
                    flat = lax.ppermute(flat, axis, pairs)
                    got, at = [], 0
                    for s in slabs:
                        got.append(flat[at:at + s.size].reshape(s.shape))
                        at += s.size
                for j, g in zip(users, got):
                    (lows if side == 0 else highs)[j].append(g)
        blocks = [
            jnp.concatenate(lows[j][::-1] + [blocks[j]] + highs[j], axis=dims[j])
            for j in range(len(blocks))
        ]
    return blocks


def inside_mask(block_shape, width):
    parts = []
    for k, axis in enumerate(AXES):
        n = block_shape[k]
        total = n * lax.axis_size(axis)
        coord = lax.axis_index(axis) * n - width + jnp.arange(n + 2 * width)
        parts.append((coord >= 0) & (coord < total))
    return parts[0][:, None, None] & parts[1][None, :, None] & parts[2][None, None, :]


def harmonic(left, right):
    return 2.0 * left * right / (left + right)


def neighbours(padded):
    return (
        padded[2:, 1:-1, 1:-1],
        padded[:-2, 1:-1, 1:-1],
        padded[1:-1, 2:, 1:-1],
        padded[1:-1, :-2, 1:-1],
        padded[1:-1, 1:-1, 2:],
        padded[1:-1, 1:-1, :-2],
    )


def face_set_zero_outside(cond):
    padded = jnp.pad(cond, 1)
    faces = tuple(harmonic(cond, jnp.where(other > 0.0, other, cond)) for other in neighbours(padded))
    diag = faces[0] + faces[1] + faces[2] + faces[3] + faces[4] + faces[5]
    return faces, diag


def operate(field, faces, diag, scale):
    near = neighbours(jnp.pad(field, 1))
    total = faces[0] * near[0] + faces[1] * near[1] + faces[2] * near[2]
    total = total + faces[3] * near[3] + faces[4] * near[4] + faces[5] * near[5]
    return scale * (diag * field - total)


def smooth(right, start, faces, diag, scale, mask=None):
    def keep(value):
        return value if mask is None else jnp.where(mask, value, 0.0)

    theta = 0.5 * (HIGH + LOW)
    delta = 0.5 * (HIGH - LOW)
    sigma = theta / delta
    rho = 1.0 / sigma
    inverse = 1.0 / (scale * diag)
    if start is None:
        resid = right
        step_dir = inverse * resid / theta
        field = keep(step_dir)
    else:
        resid = right - operate(start, faces, diag, scale)
        step_dir = inverse * resid / theta
        field = keep(start + step_dir)
    for turn in range(DEGREE - 1):
        rho_new = 1.0 / (2.0 * sigma - rho)
        resid = right - operate(field, faces, diag, scale)
        step_dir = rho_new * rho * step_dir + 2.0 * rho_new / delta * inverse * resid
        field = keep(field + step_dir)
        rho = rho_new
    return field


def restrict(field):
    field = field[0::2] + field[1::2]
    field = field[:, 0::2] + field[:, 1::2]
    field = field[:, :, 0::2] + field[:, :, 1::2]
    return field / 8.0


def prolong(field):
    return jnp.repeat(jnp.repeat(jnp.repeat(field, 2, 0), 2, 1), 2, 2)


def centre(field, width):
    return field[width:-width, width:-width, width:-width]


def face_set_global(cond):
    padded = jnp.pad(cond, 1, mode="edge")
    faces = tuple(harmonic(cond, other) for other in neighbours(padded))
    diag = faces[0] + faces[1] + faces[2] + faces[3] + faces[4] + faces[5]
    return faces, diag


def cycle_global(right, cond, level, scale):
    faces, diag = face_set_global(cond)
    if level == LEVELS:
        field = smooth(right, None, faces, diag, scale)
        return smooth(right, field, faces, diag, scale)
    field = smooth(right, None, faces, diag, scale)
    resid = right - operate(field, faces, diag, scale)
    error = cycle_global(restrict(resid), restrict(cond), level + 1, scale * 0.25)
    field = field + prolong(error)
    return smooth(right, field, faces, diag, scale)


def gather_axis(block, axis, dim):
    count = lax.axis_size(axis)
    if count & (count - 1):
        return lax.all_gather(block, axis, axis=dim, tiled=True)
    index = lax.axis_index(axis)
    step = 1
    while step < count:
        theirs = lax.ppermute(block, axis, [(i, i ^ step) for i in range(count)])
        upper = (index // step) % 2 == 1
        low = jnp.where(upper, theirs, block)
        high = jnp.where(upper, block, theirs)
        block = jnp.concatenate([low, high], axis=dim)
        step *= 2
    return block


def gather_global(block):
    block = gather_axis(block, "gz", 3)
    block = gather_axis(block, "gx", 1)
    return gather_axis(block, "gy", 2)


def local(heat_source, material, conductivity):
    cond0 = jnp.zeros(heat_source.shape, jnp.float32)
    for which in range(MATERIALS):
        cond0 = cond0 + jnp.where(material == which, conductivity[which], jnp.float32(0.0))
    cond1 = restrict(cond0)
    cond2 = restrict(cond1)
    cond3 = restrict(cond2)
    block0, block1, block2, block3 = heat_source.shape, cond1.shape, cond2.shape, cond3.shape

    ext0, cond1e, cond2e = exchange(
        [jnp.stack([cond0, heat_source]), cond1, cond2], [HALO0, HALO1, HALO2 + 1]
    )
    cond0e, right0e = ext0[0], ext0[1]

    mask0 = inside_mask(block0, HALO0)
    faces0, diag0 = face_set_zero_outside(cond0e)
    field0 = smooth(right0e, None, faces0, diag0, 1.0, mask0)
    resid0 = centre(right0e - operate(field0, faces0, diag0, 1.0), HALO0)

    faces1, diag1 = face_set_zero_outside(cond1e)
    mask1 = inside_mask(block1, HALO1)
    (right1e,) = exchange([restrict(resid0)], [HALO1])
    field1 = smooth(right1e, None, faces1, diag1, 0.25, mask1)
    resid1 = centre(right1e - operate(field1, faces1, diag1, 0.25), HALO1)

    wide2 = HALO2 + 1
    faces2, diag2 = face_set_zero_outside(cond2e)
    mask2 = inside_mask(block2, wide2)
    (right2e,) = exchange([restrict(resid1)], [HALO2])
    right2e = jnp.pad(right2e, 1)
    field2 = smooth(right2e, None, faces2, diag2, 0.0625, mask2)
    resid2 = centre(right2e - operate(field2, faces2, diag2, 0.0625), wide2)

    whole = gather_global(jnp.stack([cond3, restrict(resid2)]))
    error3 = cycle_global(whole[1], whole[0], 3, 0.015625)

    reach = wide2 // 2 + 1
    padded3 = jnp.pad(error3, reach)
    starts = [lax.axis_index(axis) * n for axis, n in zip(AXES, block3)]
    error3e = lax.dynamic_slice(padded3, starts, [n + 2 * reach for n in block3])
    error3e = centre(prolong(error3e), 2 * reach - wide2)
    field2 = jnp.where(mask2, field2 + error3e, 0.0)
    field2 = smooth(right2e, field2, faces2, diag2, 0.0625, mask2)

    cut = wide2 - HALO1 // 2
    field1 = jnp.where(mask1, field1 + prolong(field2[cut:-cut, cut:-cut, cut:-cut]), 0.0)
    field1 = smooth(right1e, field1, faces1, diag1, 0.25, mask1)

    cut = HALO1 - HALO0 // 2
    error1e = field1[cut:-cut, cut:-cut, cut:-cut]
    field0 = jnp.where(mask0, field0 + prolong(error1e), 0.0)
    field0 = smooth(right0e, field0, faces0, diag0, 1.0, mask0)
    return centre(field0, HALO0)


def solution(mesh):
    in_specs = (P("gx", "gy", "gz"), P("gx", "gy", "gz"), P())
    out_specs = P("gx", "gy", "gz")
    return jax.shard_map(local, mesh=mesh, in_specs=in_specs, out_specs=out_specs, check_vma=False)
```

```python
import jax
import jax.numpy as jnp
from jax import lax
from jax.sharding import PartitionSpec as P

DEGREE = 3
LEVELS = 3
MATERIALS = 3

LOW = 0.3
HIGH = 2.0

AXES = ("gx", "gy", "gz")
HALO0 = 6
HALO1 = 8
HALO2 = 8
BUTTERFLY = False


def exchange(blocks, widths):
    blocks = list(blocks)
    for k, axis in enumerate(AXES):
        count = lax.axis_size(axis)
        dims = [b.ndim - 3 + k for b in blocks]
        sizes = [b.shape[d] for b, d in zip(blocks, dims)]
        reach = [-(-w // n) for w, n in zip(widths, sizes)]
        lows = [[] for _ in blocks]
        highs = [[] for _ in blocks]
        for shift in range(1, max(reach) + 1):
            users = [j for j in range(len(blocks)) if reach[j] >= shift]
            takes = {j: min(sizes[j], widths[j] - (shift - 1) * sizes[j]) for j in users}
            for side in (0, 1):
                slabs = []
                for j in users:
                    n, t = sizes[j], takes[j]
                    start = n - t if side == 0 else 0
                    slabs.append(lax.slice_in_dim(blocks[j], start, start + t, axis=dims[j]))
                if shift >= count:
                    got = [jnp.zeros_like(s) for s in slabs]
                else:
                    if side == 0:
                        pairs = [(i, i + shift) for i in range(count - shift)]
                    else:
                        pairs = [(i + shift, i) for i in range(count - shift)]
                    flat = jnp.concatenate([s.reshape(-1) for s in slabs])
                    flat = lax.ppermute(flat, axis, pairs)
                    got, at = [], 0
                    for s in slabs:
                        got.append(flat[at:at + s.size].reshape(s.shape))
                        at += s.size
                for j, g in zip(users, got):
                    (lows if side == 0 else highs)[j].append(g)
        blocks = [
            jnp.concatenate(lows[j][::-1] + [blocks[j]] + highs[j], axis=dims[j])
            for j in range(len(blocks))
        ]
    return blocks


def inside_mask(block_shape, width):
    parts = []
    for k, axis in enumerate(AXES):
        n = block_shape[k]
        total = n * lax.axis_size(axis)
        coord = lax.axis_index(axis) * n - width + jnp.arange(n + 2 * width)
        parts.append((coord >= 0) & (coord < total))
    return parts[0][:, None, None] & parts[1][None, :, None] & parts[2][None, None, :]


def harmonic(left, right):
    return 2.0 * left * right / (left + right)


def neighbours(padded):
    return (
        padded[2:, 1:-1, 1:-1],
        padded[:-2, 1:-1, 1:-1],
        padded[1:-1, 2:, 1:-1],
        padded[1:-1, :-2, 1:-1],
        padded[1:-1, 1:-1, 2:],
        padded[1:-1, 1:-1, :-2],
    )


def face_set_zero_outside(cond):
    padded = jnp.pad(cond, 1)
    faces = tuple(harmonic(cond, jnp.where(other > 0.0, other, cond)) for other in neighbours(padded))
    diag = faces[0] + faces[1] + faces[2] + faces[3] + faces[4] + faces[5]
    return faces, diag


def operate(field, faces, diag, scale):
    near = neighbours(jnp.pad(field, 1))
    total = faces[0] * near[0] + faces[1] * near[1] + faces[2] * near[2]
    total = total + faces[3] * near[3] + faces[4] * near[4] + faces[5] * near[5]
    return scale * (diag * field - total)


def smooth(right, start, faces, diag, scale, mask=None):
    def keep(value):
        return value if mask is None else jnp.where(mask, value, 0.0)

    theta = 0.5 * (HIGH + LOW)
    delta = 0.5 * (HIGH - LOW)
    sigma = theta / delta
    rho = 1.0 / sigma
    inverse = 1.0 / (scale * diag)
    if start is None:
        resid = right
        step_dir = inverse * resid / theta
        field = keep(step_dir)
    else:
        resid = right - operate(start, faces, diag, scale)
        step_dir = inverse * resid / theta
        field = keep(start + step_dir)
    for turn in range(DEGREE - 1):
        rho_new = 1.0 / (2.0 * sigma - rho)
        resid = right - operate(field, faces, diag, scale)
        step_dir = rho_new * rho * step_dir + 2.0 * rho_new / delta * inverse * resid
        field = keep(field + step_dir)
        rho = rho_new
    return field


def restrict(field):
    field = field[0::2] + field[1::2]
    field = field[:, 0::2] + field[:, 1::2]
    field = field[:, :, 0::2] + field[:, :, 1::2]
    return field / 8.0


def prolong(field):
    return jnp.repeat(jnp.repeat(jnp.repeat(field, 2, 0), 2, 1), 2, 2)


def centre(field, width):
    return field[width:-width, width:-width, width:-width]


def face_set_global(cond):
    padded = jnp.pad(cond, 1, mode="edge")
    faces = tuple(harmonic(cond, other) for other in neighbours(padded))
    diag = faces[0] + faces[1] + faces[2] + faces[3] + faces[4] + faces[5]
    return faces, diag


def cycle_global(right, cond, level, scale):
    faces, diag = face_set_global(cond)
    if level == LEVELS:
        field = smooth(right, None, faces, diag, scale)
        return smooth(right, field, faces, diag, scale)
    field = smooth(right, None, faces, diag, scale)
    resid = right - operate(field, faces, diag, scale)
    error = cycle_global(restrict(resid), restrict(cond), level + 1, scale * 0.25)
    field = field + prolong(error)
    return smooth(right, field, faces, diag, scale)


def gather_axis(block, axis, dim):
    count = lax.axis_size(axis)
    if count & (count - 1) or not BUTTERFLY:
        return lax.all_gather(block, axis, axis=dim, tiled=True)
    index = lax.axis_index(axis)
    step = 1
    while step < count:
        theirs = lax.ppermute(block, axis, [(i, i ^ step) for i in range(count)])
        upper = (index // step) % 2 == 1
        low = jnp.where(upper, theirs, block)
        high = jnp.where(upper, block, theirs)
        block = jnp.concatenate([low, high], axis=dim)
        step *= 2
    return block


def gather_global(block):
    block = gather_axis(block, "gz", 3)
    block = gather_axis(block, "gx", 1)
    return gather_axis(block, "gy", 2)


def local(heat_source, material, conductivity):
    cond0 = jnp.zeros(heat_source.shape, jnp.float32)
    for which in range(MATERIALS):
        cond0 = cond0 + jnp.where(material == which, conductivity[which], jnp.float32(0.0))
    cond1 = restrict(cond0)
    cond2 = restrict(cond1)
    cond3 = restrict(cond2)
    block0, block1, block2, block3 = heat_source.shape, cond1.shape, cond2.shape, cond3.shape

    ext0, cond1e, cond2e = exchange(
        [jnp.stack([cond0, heat_source]), cond1, cond2], [HALO0, HALO1, HALO2 + 1]
    )
    cond0e, right0e = ext0[0], ext0[1]

    mask0 = inside_mask(block0, HALO0)
    faces0, diag0 = face_set_zero_outside(cond0e)
    field0 = smooth(right0e, None, faces0, diag0, 1.0, mask0)
    resid0 = centre(right0e - operate(field0, faces0, diag0, 1.0), HALO0)

    faces1, diag1 = face_set_zero_outside(cond1e)
    mask1 = inside_mask(block1, HALO1)
    (right1e,) = exchange([restrict(resid0)], [HALO1])
    field1 = smooth(right1e, None, faces1, diag1, 0.25, mask1)
    resid1 = centre(right1e - operate(field1, faces1, diag1, 0.25), HALO1)

    wide2 = HALO2 + 1
    faces2, diag2 = face_set_zero_outside(cond2e)
    mask2 = inside_mask(block2, wide2)
    (right2e,) = exchange([restrict(resid1)], [HALO2])
    right2e = jnp.pad(right2e, 1)
    field2 = smooth(right2e, None, faces2, diag2, 0.0625, mask2)
    resid2 = centre(right2e - operate(field2, faces2, diag2, 0.0625), wide2)

    whole = gather_global(jnp.stack([cond3, restrict(resid2)]))
    error3 = cycle_global(whole[1], whole[0], 3, 0.015625)

    reach = wide2 // 2 + 1
    padded3 = jnp.pad(error3, reach)
    starts = [lax.axis_index(axis) * n for axis, n in zip(AXES, block3)]
    error3e = lax.dynamic_slice(padded3, starts, [n + 2 * reach for n in block3])
    error3e = centre(prolong(error3e), 2 * reach - wide2)
    field2 = jnp.where(mask2, field2 + error3e, 0.0)
    field2 = smooth(right2e, field2, faces2, diag2, 0.0625, mask2)

    cut = wide2 - HALO1 // 2
    field1 = jnp.where(mask1, field1 + prolong(field2[cut:-cut, cut:-cut, cut:-cut]), 0.0)
    field1 = smooth(right1e, field1, faces1, diag1, 0.25, mask1)

    cut = HALO1 - HALO0 // 2
    error1e = field1[cut:-cut, cut:-cut, cut:-cut]
    field0 = jnp.where(mask0, field0 + prolong(error1e), 0.0)
    field0 = smooth(right0e, field0, faces0, diag0, 1.0, mask0)
    return centre(field0, HALO0)


def solution(mesh):
    in_specs = (P("gx", "gy", "gz"), P("gx", "gy", "gz"), P())
    out_specs = P("gx", "gy", "gz")
    return jax.shard_map(local, mesh=mesh, in_specs=in_specs, out_specs=out_specs, check_vma=False)
```

```python
import jax
import jax.numpy as jnp
from jax import lax
from jax.sharding import PartitionSpec as P

DEGREE = 3
LEVELS = 3
MATERIALS = 3

LOW = 0.3
HIGH = 2.0

AXES = ("gx", "gy", "gz")
HALO0 = 6
HALO1 = 8


def exchange(block, width):
    for k, axis in enumerate(AXES):
        dim = block.ndim - 3 + k
        count = lax.axis_size(axis)
        forward = [(i, i + 1) for i in range(count - 1)]
        backward = [(i + 1, i) for i in range(count - 1)]
        size = block.shape[dim]
        low = lax.ppermute(lax.slice_in_dim(block, size - width, size, axis=dim), axis, forward)
        high = lax.ppermute(lax.slice_in_dim(block, 0, width, axis=dim), axis, backward)
        block = jnp.concatenate([low, block, high], axis=dim)
    return block


def inside_mask(block_shape, width):
    parts = []
    for k, axis in enumerate(AXES):
        n = block_shape[k]
        total = n * lax.axis_size(axis)
        coord = lax.axis_index(axis) * n - width + jnp.arange(n + 2 * width)
        parts.append((coord >= 0) & (coord < total))
    return parts[0][:, None, None] & parts[1][None, :, None] & parts[2][None, None, :]


def harmonic(left, right):
    return 2.0 * left * right / (left + right)


def neighbours(padded):
    return (
        padded[2:, 1:-1, 1:-1],
        padded[:-2, 1:-1, 1:-1],
        padded[1:-1, 2:, 1:-1],
        padded[1:-1, :-2, 1:-1],
        padded[1:-1, 1:-1, 2:],
        padded[1:-1, 1:-1, :-2],
    )


def face_set_zero_outside(cond):
    padded = jnp.pad(cond, 1)
    faces = tuple(harmonic(cond, jnp.where(other > 0.0, other, cond)) for other in neighbours(padded))
    diag = faces[0] + faces[1] + faces[2] + faces[3] + faces[4] + faces[5]
    return faces, diag


def operate(field, faces, diag, scale):
    near = neighbours(jnp.pad(field, 1))
    total = faces[0] * near[0] + faces[1] * near[1] + faces[2] * near[2]
    total = total + faces[3] * near[3] + faces[4] * near[4] + faces[5] * near[5]
    return scale * (diag * field - total)


def smooth(right, start, faces, diag, scale, mask=None):
    def keep(value):
        return value if mask is None else jnp.where(mask, value, 0.0)

    theta = 0.5 * (HIGH + LOW)
    delta = 0.5 * (HIGH - LOW)
    sigma = theta / delta
    rho = 1.0 / sigma
    inverse = 1.0 / (scale * diag)
    if start is None:
        resid = right
        step_dir = inverse * resid / theta
        field = keep(step_dir)
    else:
        resid = right - operate(start, faces, diag, scale)
        step_dir = inverse * resid / theta
        field = keep(start + step_dir)
    for turn in range(DEGREE - 1):
        rho_new = 1.0 / (2.0 * sigma - rho)
        resid = right - operate(field, faces, diag, scale)
        step_dir = rho_new * rho * step_dir + 2.0 * rho_new / delta * inverse * resid
        field = keep(field + step_dir)
        rho = rho_new
    return field


def restrict(field):
    field = field[0::2] + field[1::2]
    field = field[:, 0::2] + field[:, 1::2]
    sx, sy, sz = field.shape
    pairs = (jnp.arange(sz)[:, None] // 2 == jnp.arange(sz // 2)[None, :]).astype(field.dtype)
    field = jnp.dot(field.reshape(sx * sy, sz), pairs, precision=lax.Precision.HIGHEST)
    return field.reshape(sx, sy, sz // 2) / 8.0


def prolong(field):
    return jnp.repeat(jnp.repeat(jnp.repeat(field, 2, 0), 2, 1), 2, 2)


def centre(field, width):
    return field[width:-width, width:-width, width:-width]


def face_set_global(cond):
    padded = jnp.pad(cond, 1, mode="edge")
    faces = tuple(harmonic(cond, other) for other in neighbours(padded))
    diag = faces[0] + faces[1] + faces[2] + faces[3] + faces[4] + faces[5]
    return faces, diag


def cycle_global(right, cond, level, scale):
    faces, diag = face_set_global(cond)
    if level == LEVELS:
        field = smooth(right, None, faces, diag, scale)
        return smooth(right, field, faces, diag, scale)
    field = smooth(right, None, faces, diag, scale)
    resid = right - operate(field, faces, diag, scale)
    error = cycle_global(restrict(resid), restrict(cond), level + 1, scale * 0.25)
    field = field + prolong(error)
    return smooth(right, field, faces, diag, scale)


def gather_axis(block, axis, dim, descending=False):
    count = lax.axis_size(axis)
    if count & (count - 1):
        return lax.all_gather(block, axis, axis=dim, tiled=True)
    index = lax.axis_index(axis)
    steps = []
    step = 1
    while step < count:
        steps.append(step)
        step *= 2
    if descending:
        steps = steps[::-1]
    size = block.shape[dim]
    for step in steps:
        theirs = lax.ppermute(block, axis, [(i, i ^ step) for i in range(count)])
        upper = (index // step) % 2 == 1
        low = jnp.where(upper, theirs, block)
        high = jnp.where(upper, block, theirs)
        block = jnp.concatenate([low, high], axis=dim)
    if descending and len(steps) > 1:
        bits = len(steps)
        shape = block.shape
        split = shape[:dim] + (2,) * bits + (size,) + shape[dim + 1:]
        order = (
            list(range(dim))
            + [dim + bits - 1 - b for b in range(bits)]
            + list(range(dim + bits, len(split)))
        )
        block = block.reshape(split).transpose(order).reshape(shape)
    return block


def gather_global(block):
    block = gather_axis(block, "gz", 3)
    block = gather_axis(block, "gy", 2)
    return gather_axis(block, "gx", 1, descending=True)


def local(heat_source, material, conductivity):
    cond0 = jnp.zeros(heat_source.shape, jnp.float32)
    for which in range(MATERIALS):
        cond0 = cond0 + jnp.where(material == which, conductivity[which], jnp.float32(0.0))
    cond1 = restrict(cond0)
    cond2 = restrict(cond1)
    block0, block1 = heat_source.shape, cond1.shape

    ext0 = exchange(jnp.stack([cond0, heat_source]), HALO0)
    cond0e, right0e = ext0[0], ext0[1]
    mask0 = inside_mask(block0, HALO0)
    faces0, diag0 = face_set_zero_outside(cond0e)
    field0 = smooth(right0e, None, faces0, diag0, 1.0, mask0)
    resid0 = centre(right0e - operate(field0, faces0, diag0, 1.0), HALO0)

    cond1e = exchange(cond1, HALO1)
    faces1, diag1 = face_set_zero_outside(cond1e)
    mask1 = inside_mask(block1, HALO1)
    right1e = exchange(restrict(resid0), HALO1)
    field1 = smooth(right1e, None, faces1, diag1, 0.25, mask1)
    resid1 = centre(right1e - operate(field1, faces1, diag1, 0.25), HALO1)

    whole = gather_global(jnp.stack([cond2, restrict(resid1)]))
    error2 = cycle_global(whole[1], whole[0], 2, 0.0625)

    reach = HALO1 // 2
    padded2 = jnp.pad(error2, reach)
    block2 = cond2.shape
    starts = [lax.axis_index(axis) * n for axis, n in zip(AXES, block2)]
    sizes = [n + 2 * reach for n in block2]
    error2e = lax.dynamic_slice(padded2, starts, sizes)
    field1 = jnp.where(mask1, field1 + prolong(error2e), 0.0)
    field1 = smooth(right1e, field1, faces1, diag1, 0.25, mask1)

    cut = HALO1 - HALO0 // 2
    error1e = field1[cut:-cut, cut:-cut, cut:-cut]
    field0 = jnp.where(mask0, field0 + prolong(error1e), 0.0)
    field0 = smooth(right0e, field0, faces0, diag0, 1.0, mask0)
    return centre(field0, HALO0)


def solution(mesh):
    in_specs = (P("gx", "gy", "gz"), P("gx", "gy", "gz"), P())
    out_specs = P("gx", "gy", "gz")
    return jax.shard_map(local, mesh=mesh, in_specs=in_specs, out_specs=out_specs, check_vma=False)
```

```python
import jax
import jax.numpy as jnp
from jax import lax
from jax.sharding import PartitionSpec as P

DEGREE = 3
LEVELS = 3
MATERIALS = 3

LOW = 0.3
HIGH = 2.0

AXES = ("gx", "gy", "gz")
HALO0 = 6
HALO1 = 8


def exchange(block, width):
    for k, axis in enumerate(AXES):
        dim = block.ndim - 3 + k
        count = lax.axis_size(axis)
        forward = [(i, i + 1) for i in range(count - 1)]
        backward = [(i + 1, i) for i in range(count - 1)]
        size = block.shape[dim]
        low = lax.ppermute(lax.slice_in_dim(block, size - width, size, axis=dim), axis, forward)
        high = lax.ppermute(lax.slice_in_dim(block, 0, width, axis=dim), axis, backward)
        block = jnp.concatenate([low, block, high], axis=dim)
    return block


def inside_mask(block_shape, width):
    parts = []
    for k, axis in enumerate(AXES):
        n = block_shape[k]
        total = n * lax.axis_size(axis)
        coord = lax.axis_index(axis) * n - width + jnp.arange(n + 2 * width)
        parts.append((coord >= 0) & (coord < total))
    return parts[0][:, None, None] & parts[1][None, :, None] & parts[2][None, None, :]


def harmonic(left, right):
    return 2.0 * left * right / (left + right)


def neighbours(padded):
    return (
        padded[2:, 1:-1, 1:-1],
        padded[:-2, 1:-1, 1:-1],
        padded[1:-1, 2:, 1:-1],
        padded[1:-1, :-2, 1:-1],
        padded[1:-1, 1:-1, 2:],
        padded[1:-1, 1:-1, :-2],
    )


def face_set_zero_outside(cond):
    padded = jnp.pad(cond, 1)
    faces = tuple(harmonic(cond, jnp.where(other > 0.0, other, cond)) for other in neighbours(padded))
    diag = faces[0] + faces[1] + faces[2] + faces[3] + faces[4] + faces[5]
    return faces, diag


def operate(field, faces, diag, scale):
    near = neighbours(jnp.pad(field, 1))
    total = faces[0] * near[0] + faces[1] * near[1] + faces[2] * near[2]
    total = total + faces[3] * near[3] + faces[4] * near[4] + faces[5] * near[5]
    return scale * (diag * field - total)


def smooth(right, start, faces, diag, scale, mask=None):
    def keep(value):
        return value if mask is None else jnp.where(mask, value, 0.0)

    theta = 0.5 * (HIGH + LOW)
    delta = 0.5 * (HIGH - LOW)
    sigma = theta / delta
    rho = 1.0 / sigma
    inverse = 1.0 / (scale * diag)
    if start is None:
        resid = right
        step_dir = inverse * resid / theta
        field = keep(step_dir)
    else:
        resid = right - operate(start, faces, diag, scale)
        step_dir = inverse * resid / theta
        field = keep(start + step_dir)
    for turn in range(DEGREE - 1):
        rho_new = 1.0 / (2.0 * sigma - rho)
        resid = right - operate(field, faces, diag, scale)
        step_dir = rho_new * rho * step_dir + 2.0 * rho_new / delta * inverse * resid
        field = keep(field + step_dir)
        rho = rho_new
    return field


def restrict(field):
    field = field[0::2] + field[1::2]
    field = field[:, 0::2] + field[:, 1::2]
    field = field[:, :, 0::2] + field[:, :, 1::2]
    return field / 8.0


def prolong(field):
    return jnp.repeat(jnp.repeat(jnp.repeat(field, 2, 0), 2, 1), 2, 2)


def centre(field, width):
    return field[width:-width, width:-width, width:-width]


def face_set_global(cond):
    padded = jnp.pad(cond, 1, mode="edge")
    faces = tuple(harmonic(cond, other) for other in neighbours(padded))
    diag = faces[0] + faces[1] + faces[2] + faces[3] + faces[4] + faces[5]
    return faces, diag


def cycle_global(right, cond, level, scale):
    faces, diag = face_set_global(cond)
    if level == LEVELS:
        field = smooth(right, None, faces, diag, scale)
        return smooth(right, field, faces, diag, scale)
    field = smooth(right, None, faces, diag, scale)
    resid = right - operate(field, faces, diag, scale)
    error = cycle_global(restrict(resid), restrict(cond), level + 1, scale * 0.25)
    field = field + prolong(error)
    return smooth(right, field, faces, diag, scale)


def gather_axis(block, axis, dim, descending=False):
    count = lax.axis_size(axis)
    if count & (count - 1):
        return lax.all_gather(block, axis, axis=dim, tiled=True)
    index = lax.axis_index(axis)
    steps = []
    step = 1
    while step < count:
        steps.append(step)
        step *= 2
    if descending:
        steps = steps[::-1]
    size = block.shape[dim]
    for step in steps:
        theirs = lax.ppermute(block, axis, [(i, i ^ step) for i in range(count)])
        upper = (index // step) % 2 == 1
        low = jnp.where(upper, theirs, block)
        high = jnp.where(upper, block, theirs)
        block = jnp.concatenate([low, high], axis=dim)
    if descending and len(steps) > 1:
        bits = len(steps)
        shape = block.shape
        split = shape[:dim] + (2,) * bits + (size,) + shape[dim + 1:]
        order = (
            list(range(dim))
            + [dim + bits - 1 - b for b in range(bits)]
            + list(range(dim + bits, len(split)))
        )
        block = block.reshape(split).transpose(order).reshape(shape)
    return block


def gather_global(block):
    block = gather_axis(block, "gz", 3)
    block = gather_axis(block, "gy", 2)
    return gather_axis(block, "gx", 1, descending=True)


def local(heat_source, material, conductivity):
    cond0 = jnp.zeros(heat_source.shape, jnp.float32)
    for which in range(MATERIALS):
        cond0 = cond0 + jnp.where(material == which, conductivity[which], jnp.float32(0.0))
    cond1 = restrict(cond0)
    cond2 = restrict(cond1)
    block0, block1 = heat_source.shape, cond1.shape

    ext0 = exchange(jnp.stack([cond0, heat_source]), HALO0)
    cond0e, right0e = ext0[0], ext0[1]
    mask0 = inside_mask(block0, HALO0)
    faces0, diag0 = face_set_zero_outside(cond0e)
    field0 = smooth(right0e, None, faces0, diag0, 1.0, mask0)
    resid0 = centre(right0e - operate(field0, faces0, diag0, 1.0), HALO0)

    cond1e = exchange(cond1, HALO1)
    faces1, diag1 = face_set_zero_outside(cond1e)
    mask1 = inside_mask(block1, HALO1)
    right1e = exchange(restrict(resid0), HALO1)
    field1 = smooth(right1e, None, faces1, diag1, 0.25, mask1)
    resid1 = centre(right1e - operate(field1, faces1, diag1, 0.25), HALO1)

    whole = gather_global(jnp.stack([cond2, restrict(resid1)]))
    error2 = cycle_global(whole[1], whole[0], 2, 0.0625)

    reach = HALO1 // 2
    padded2 = jnp.pad(error2, reach)
    block2 = cond2.shape
    starts = [lax.axis_index(axis) * n for axis, n in zip(AXES, block2)]
    sizes = [n + 2 * reach for n in block2]
    error2e = lax.dynamic_slice(padded2, starts, sizes)
    field1 = jnp.where(mask1, field1 + prolong(error2e), 0.0)
    field1 = smooth(right1e, field1, faces1, diag1, 0.25, mask1)

    cut = HALO1 - HALO0 // 2
    error1e = field1[cut:-cut, cut:-cut, cut:-cut]
    field0 = jnp.where(mask0, field0 + prolong(error1e), 0.0)
    field0 = smooth(right0e, field0, faces0, diag0, 1.0, mask0)
    return centre(field0, HALO0)


def solution(mesh):
    in_specs = (P("gx", "gy", "gz"), P("gx", "gy", "gz"), P())
    out_specs = P("gx", "gy", "gz")
    return jax.shard_map(local, mesh=mesh, in_specs=in_specs, out_specs=out_specs, check_vma=False)
```

```python
import jax
import jax.numpy as jnp
from jax import lax
from jax.sharding import PartitionSpec as P

DEGREE = 3
LEVELS = 3
MATERIALS = 3

LOW = 0.3
HIGH = 2.0

AXES = ("gx", "gy", "gz")
HALO0 = 6
HALO1 = 8


def exchange(blocks, widths):
    blocks = list(blocks)
    for k, axis in enumerate(AXES):
        count = lax.axis_size(axis)
        dims = [b.ndim - 3 + k for b in blocks]
        sizes = [b.shape[d] for b, d in zip(blocks, dims)]
        reach = [-(-w // n) for w, n in zip(widths, sizes)]
        lows = [[] for _ in blocks]
        highs = [[] for _ in blocks]
        for shift in range(1, max(reach) + 1):
            users = [j for j in range(len(blocks)) if reach[j] >= shift]
            takes = {j: min(sizes[j], widths[j] - (shift - 1) * sizes[j]) for j in users}
            for side in (0, 1):
                slabs = []
                for j in users:
                    n, t = sizes[j], takes[j]
                    start = n - t if side == 0 else 0
                    slabs.append(lax.slice_in_dim(blocks[j], start, start + t, axis=dims[j]))
                if shift >= count:
                    got = [jnp.zeros_like(s) for s in slabs]
                else:
                    if side == 0:
                        pairs = [(i, i + shift) for i in range(count - shift)]
                    else:
                        pairs = [(i + shift, i) for i in range(count - shift)]
                    flat = jnp.concatenate([s.reshape(-1) for s in slabs])
                    flat = lax.ppermute(flat, axis, pairs)
                    got, at = [], 0
                    for s in slabs:
                        got.append(flat[at:at + s.size].reshape(s.shape))
                        at += s.size
                for j, g in zip(users, got):
                    (lows if side == 0 else highs)[j].append(g)
        blocks = [
            jnp.concatenate(lows[j][::-1] + [blocks[j]] + highs[j], axis=dims[j])
            for j in range(len(blocks))
        ]
    return blocks


def inside_mask(block_shape, width):
    parts = []
    for k, axis in enumerate(AXES):
        n = block_shape[k]
        total = n * lax.axis_size(axis)
        coord = lax.axis_index(axis) * n - width + jnp.arange(n + 2 * width)
        parts.append((coord >= 0) & (coord < total))
    return parts[0][:, None, None] & parts[1][None, :, None] & parts[2][None, None, :]


def harmonic(left, right):
    return 2.0 * left * right / (left + right)


def neighbours(padded):
    return (
        padded[2:, 1:-1, 1:-1],
        padded[:-2, 1:-1, 1:-1],
        padded[1:-1, 2:, 1:-1],
        padded[1:-1, :-2, 1:-1],
        padded[1:-1, 1:-1, 2:],
        padded[1:-1, 1:-1, :-2],
    )


def face_set_zero_outside(cond):
    padded = jnp.pad(cond, 1)
    faces = tuple(harmonic(cond, jnp.where(other > 0.0, other, cond)) for other in neighbours(padded))
    diag = faces[0] + faces[1] + faces[2] + faces[3] + faces[4] + faces[5]
    return faces, diag


def operate(field, faces, diag, scale):
    near = neighbours(jnp.pad(field, 1))
    total = faces[0] * near[0] + faces[1] * near[1] + faces[2] * near[2]
    total = total + faces[3] * near[3] + faces[4] * near[4] + faces[5] * near[5]
    return scale * (diag * field - total)


def smooth(right, start, faces, diag, scale, mask=None):
    def keep(value):
        return value if mask is None else jnp.where(mask, value, 0.0)

    theta = 0.5 * (HIGH + LOW)
    delta = 0.5 * (HIGH - LOW)
    sigma = theta / delta
    rho = 1.0 / sigma
    inverse = 1.0 / (scale * diag)
    if start is None:
        resid = right
        step_dir = inverse * resid / theta
        field = keep(step_dir)
    else:
        resid = right - operate(start, faces, diag, scale)
        step_dir = inverse * resid / theta
        field = keep(start + step_dir)
    for turn in range(DEGREE - 1):
        rho_new = 1.0 / (2.0 * sigma - rho)
        resid = right - operate(field, faces, diag, scale)
        step_dir = rho_new * rho * step_dir + 2.0 * rho_new / delta * inverse * resid
        field = keep(field + step_dir)
        rho = rho_new
    return field


def restrict(field):
    field = field[0::2] + field[1::2]
    field = field[:, 0::2] + field[:, 1::2]
    field = field[:, :, 0::2] + field[:, :, 1::2]
    return field / 8.0


def prolong(field):
    return jnp.repeat(jnp.repeat(jnp.repeat(field, 2, 0), 2, 1), 2, 2)


def centre(field, width):
    return field[width:-width, width:-width, width:-width]


def face_set_global(cond):
    padded = jnp.pad(cond, 1, mode="edge")
    faces = tuple(harmonic(cond, other) for other in neighbours(padded))
    diag = faces[0] + faces[1] + faces[2] + faces[3] + faces[4] + faces[5]
    return faces, diag


def cycle_global(right, cond, level, scale):
    faces, diag = face_set_global(cond)
    if level == LEVELS:
        field = smooth(right, None, faces, diag, scale)
        return smooth(right, field, faces, diag, scale)
    field = smooth(right, None, faces, diag, scale)
    resid = right - operate(field, faces, diag, scale)
    error = cycle_global(restrict(resid), restrict(cond), level + 1, scale * 0.25)
    field = field + prolong(error)
    return smooth(right, field, faces, diag, scale)


def gather_axis(block, axis, dim, descending=False):
    count = lax.axis_size(axis)
    if count & (count - 1):
        return lax.all_gather(block, axis, axis=dim, tiled=True)
    index = lax.axis_index(axis)
    steps = []
    step = 1
    while step < count:
        steps.append(step)
        step *= 2
    if descending:
        steps = steps[::-1]
    size = block.shape[dim]
    for step in steps:
        theirs = lax.ppermute(block, axis, [(i, i ^ step) for i in range(count)])
        upper = (index // step) % 2 == 1
        low = jnp.where(upper, theirs, block)
        high = jnp.where(upper, block, theirs)
        block = jnp.concatenate([low, high], axis=dim)
    if descending and len(steps) > 1:
        bits = len(steps)
        shape = block.shape
        split = shape[:dim] + (2,) * bits + (size,) + shape[dim + 1:]
        order = (
            list(range(dim))
            + [dim + bits - 1 - b for b in range(bits)]
            + list(range(dim + bits, len(split)))
        )
        block = block.reshape(split).transpose(order).reshape(shape)
    return block


def gather_global(block):
    block = gather_axis(block, "gz", 3)
    block = gather_axis(block, "gy", 2)
    return gather_axis(block, "gx", 1, descending=True)


def local(heat_source, material, conductivity):
    cond0 = jnp.zeros(heat_source.shape, jnp.float32)
    for which in range(MATERIALS):
        cond0 = cond0 + jnp.where(material == which, conductivity[which], jnp.float32(0.0))
    cond1 = restrict(cond0)
    cond2 = restrict(cond1)
    block0, block1 = heat_source.shape, cond1.shape

    ext0, cond1e = exchange([jnp.stack([cond0, heat_source]), cond1], [HALO0, HALO1])
    cond0e, right0e = ext0[0], ext0[1]

    mask0 = inside_mask(block0, HALO0)
    faces0, diag0 = face_set_zero_outside(cond0e)
    field0 = smooth(right0e, None, faces0, diag0, 1.0, mask0)
    resid0 = centre(right0e - operate(field0, faces0, diag0, 1.0), HALO0)

    faces1, diag1 = face_set_zero_outside(cond1e)
    mask1 = inside_mask(block1, HALO1)
    (right1e,) = exchange([restrict(resid0)], [HALO1])
    field1 = smooth(right1e, None, faces1, diag1, 0.25, mask1)
    resid1 = centre(right1e - operate(field1, faces1, diag1, 0.25), HALO1)

    whole = gather_global(jnp.stack([cond2, restrict(resid1)]))
    error2 = cycle_global(whole[1], whole[0], 2, 0.0625)

    reach = HALO1 // 2
    padded2 = jnp.pad(error2, reach)
    block2 = cond2.shape
    starts = [lax.axis_index(axis) * n for axis, n in zip(AXES, block2)]
    sizes = [n + 2 * reach for n in block2]
    error2e = lax.dynamic_slice(padded2, starts, sizes)
    field1 = jnp.where(mask1, field1 + prolong(error2e), 0.0)
    field1 = smooth(right1e, field1, faces1, diag1, 0.25, mask1)

    cut = HALO1 - HALO0 // 2
    error1e = field1[cut:-cut, cut:-cut, cut:-cut]
    field0 = jnp.where(mask0, field0 + prolong(error1e), 0.0)
    field0 = smooth(right0e, field0, faces0, diag0, 1.0, mask0)
    return centre(field0, HALO0)


def solution(mesh):
    in_specs = (P("gx", "gy", "gz"), P("gx", "gy", "gz"), P())
    out_specs = P("gx", "gy", "gz")
    return jax.shard_map(local, mesh=mesh, in_specs=in_specs, out_specs=out_specs, check_vma=False)
```

```python
import jax
import jax.numpy as jnp
from jax import lax
from jax.sharding import PartitionSpec as P

DEGREE = 3
LEVELS = 3
MATERIALS = 3

LOW = 0.3
HIGH = 2.0

AXES = ("gx", "gy", "gz")
HALO0 = 6
HALO1 = 8


def exchange(blocks, widths):
    blocks = list(blocks)
    for k, axis in enumerate(AXES):
        count = lax.axis_size(axis)
        dims = [b.ndim - 3 + k for b in blocks]
        sizes = [b.shape[d] for b, d in zip(blocks, dims)]
        reach = [-(-w // n) for w, n in zip(widths, sizes)]
        lows = [[] for _ in blocks]
        highs = [[] for _ in blocks]
        for shift in range(1, max(reach) + 1):
            users = [j for j in range(len(blocks)) if reach[j] >= shift]
            takes = {j: min(sizes[j], widths[j] - (shift - 1) * sizes[j]) for j in users}
            for side in (0, 1):
                slabs = []
                for j in users:
                    n, t = sizes[j], takes[j]
                    start = n - t if side == 0 else 0
                    slabs.append(lax.slice_in_dim(blocks[j], start, start + t, axis=dims[j]))
                if shift >= count:
                    got = [jnp.zeros_like(s) for s in slabs]
                else:
                    if side == 0:
                        pairs = [(i, i + shift) for i in range(count - shift)]
                    else:
                        pairs = [(i + shift, i) for i in range(count - shift)]
                    flat = jnp.concatenate([s.reshape(-1) for s in slabs])
                    flat = lax.ppermute(flat, axis, pairs)
                    got, at = [], 0
                    for s in slabs:
                        got.append(flat[at:at + s.size].reshape(s.shape))
                        at += s.size
                for j, g in zip(users, got):
                    (lows if side == 0 else highs)[j].append(g)
        blocks = [
            jnp.concatenate(lows[j][::-1] + [blocks[j]] + highs[j], axis=dims[j])
            for j in range(len(blocks))
        ]
    return blocks


def inside_mask(block_shape, width):
    parts = []
    for k, axis in enumerate(AXES):
        n = block_shape[k]
        total = n * lax.axis_size(axis)
        coord = lax.axis_index(axis) * n - width + jnp.arange(n + 2 * width)
        parts.append((coord >= 0) & (coord < total))
    return parts[0][:, None, None] & parts[1][None, :, None] & parts[2][None, None, :]


def harmonic(left, right):
    return 2.0 * left * right / (left + right)


def neighbours(padded):
    return (
        padded[2:, 1:-1, 1:-1],
        padded[:-2, 1:-1, 1:-1],
        padded[1:-1, 2:, 1:-1],
        padded[1:-1, :-2, 1:-1],
        padded[1:-1, 1:-1, 2:],
        padded[1:-1, 1:-1, :-2],
    )


def face_set_zero_outside(cond):
    padded = jnp.pad(cond, 1)
    faces = tuple(harmonic(cond, jnp.where(other > 0.0, other, cond)) for other in neighbours(padded))
    diag = faces[0] + faces[1] + faces[2] + faces[3] + faces[4] + faces[5]
    return faces, diag


def operate(field, faces, diag, scale):
    near = neighbours(jnp.pad(field, 1))
    total = faces[0] * near[0] + faces[1] * near[1] + faces[2] * near[2]
    total = total + faces[3] * near[3] + faces[4] * near[4] + faces[5] * near[5]
    return scale * (diag * field - total)


def smooth(right, start, faces, diag, scale, mask=None, operate=operate):
    def keep(value):
        return value if mask is None else jnp.where(mask, value, 0.0)

    theta = 0.5 * (HIGH + LOW)
    delta = 0.5 * (HIGH - LOW)
    sigma = theta / delta
    rho = 1.0 / sigma
    inverse = 1.0 / (scale * diag)
    if start is None:
        resid = right
        step_dir = inverse * resid / theta
        field = keep(step_dir)
    else:
        resid = right - operate(start, faces, diag, scale)
        step_dir = inverse * resid / theta
        field = keep(start + step_dir)
    for turn in range(DEGREE - 1):
        rho_new = 1.0 / (2.0 * sigma - rho)
        resid = right - operate(field, faces, diag, scale)
        step_dir = rho_new * rho * step_dir + 2.0 * rho_new / delta * inverse * resid
        field = keep(field + step_dir)
        rho = rho_new
    return field


def restrict(field):
    field = field[0::2] + field[1::2]
    field = field[:, 0::2] + field[:, 1::2]
    field = field[:, :, 0::2] + field[:, :, 1::2]
    return field / 8.0


def prolong(field):
    return jnp.repeat(jnp.repeat(jnp.repeat(field, 2, 0), 2, 1), 2, 2)


def centre(field, width):
    return field[width:-width, width:-width, width:-width]


def face_set_global(cond):
    padded = jnp.pad(cond, 1, mode="edge")
    faces = tuple(harmonic(cond, other) for other in neighbours(padded))
    diag = faces[0] + faces[1] + faces[2] + faces[3] + faces[4] + faces[5]
    return faces, diag


def neighbours_dilated(padded):
    return (
        padded[2:, 1:-1, 2:-2],
        padded[:-2, 1:-1, 2:-2],
        padded[1:-1, 2:, 2:-2],
        padded[1:-1, :-2, 2:-2],
        padded[1:-1, 1:-1, 4:],
        padded[1:-1, 1:-1, :-4],
    )


def face_set_dilated(cond):
    padded = jnp.concatenate([cond[:, :, :2], cond, cond[:, :, -2:]], axis=2)
    padded = jnp.pad(padded, ((1, 1), (1, 1), (0, 0)), mode="edge")
    faces = tuple(harmonic(cond, other) for other in neighbours_dilated(padded))
    diag = faces[0] + faces[1] + faces[2] + faces[3] + faces[4] + faces[5]
    return faces, diag


def operate_dilated(field, faces, diag, scale):
    near = neighbours_dilated(jnp.pad(field, ((1, 1), (1, 1), (2, 2))))
    total = faces[0] * near[0] + faces[1] * near[1] + faces[2] * near[2]
    total = total + faces[3] * near[3] + faces[4] * near[4] + faces[5] * near[5]
    return scale * (diag * field - total)


def restrict_dilated(field):
    field = field[0::2] + field[1::2]
    field = field[:, 0::2] + field[:, 1::2]
    later = jnp.concatenate([field[:, :, 1:], jnp.zeros_like(field[:, :, :1])], axis=2)
    return (field + later) / 8.0


def prolong_dilated(field):
    earlier = jnp.concatenate([jnp.zeros_like(field[:, :, :1]), field[:, :, :-1]], axis=2)
    odd = (jnp.arange(field.shape[2]) % 2 == 1)[None, None, :]
    field = jnp.where(odd, earlier, field)
    return jnp.repeat(jnp.repeat(field, 2, 0), 2, 1)


def cycle_global(right, cond, scale):
    faces, diag = face_set_global(cond)
    field = smooth(right, None, faces, diag, scale)
    resid = right - operate(field, faces, diag, scale)
    right3, cond3 = restrict_dilated(resid), restrict_dilated(cond)
    faces3, diag3 = face_set_dilated(cond3)
    scale3 = scale * 0.25
    error = smooth(right3, None, faces3, diag3, scale3, operate=operate_dilated)
    error = smooth(right3, error, faces3, diag3, scale3, operate=operate_dilated)
    field = field + prolong_dilated(error)
    return smooth(right, field, faces, diag, scale)


def gather_axis(block, axis, dim, descending=False):
    count = lax.axis_size(axis)
    if count & (count - 1):
        return lax.all_gather(block, axis, axis=dim, tiled=True)
    index = lax.axis_index(axis)
    steps = []
    step = 1
    while step < count:
        steps.append(step)
        step *= 2
    if descending:
        steps = steps[::-1]
    size = block.shape[dim]
    for step in steps:
        theirs = lax.ppermute(block, axis, [(i, i ^ step) for i in range(count)])
        upper = (index // step) % 2 == 1
        low = jnp.where(upper, theirs, block)
        high = jnp.where(upper, block, theirs)
        block = jnp.concatenate([low, high], axis=dim)
    if descending and len(steps) > 1:
        bits = len(steps)
        shape = block.shape
        split = shape[:dim] + (2,) * bits + (size,) + shape[dim + 1:]
        order = (
            list(range(dim))
            + [dim + bits - 1 - b for b in range(bits)]
            + list(range(dim + bits, len(split)))
        )
        block = block.reshape(split).transpose(order).reshape(shape)
    return block


def gather_global(block):
    block = gather_axis(block, "gz", 3)
    block = gather_axis(block, "gy", 2)
    return gather_axis(block, "gx", 1, descending=True)


def local(heat_source, material, conductivity):
    cond0 = jnp.zeros(heat_source.shape, jnp.float32)
    for which in range(MATERIALS):
        cond0 = cond0 + jnp.where(material == which, conductivity[which], jnp.float32(0.0))
    cond1 = restrict(cond0)
    cond2 = restrict(cond1)
    block0, block1 = heat_source.shape, cond1.shape

    ext0, cond1e = exchange([jnp.stack([cond0, heat_source]), cond1], [HALO0, HALO1])
    cond0e, right0e = ext0[0], ext0[1]

    mask0 = inside_mask(block0, HALO0)
    faces0, diag0 = face_set_zero_outside(cond0e)
    field0 = smooth(right0e, None, faces0, diag0, 1.0, mask0)
    resid0 = centre(right0e - operate(field0, faces0, diag0, 1.0), HALO0)

    faces1, diag1 = face_set_zero_outside(cond1e)
    mask1 = inside_mask(block1, HALO1)
    (right1e,) = exchange([restrict(resid0)], [HALO1])
    field1 = smooth(right1e, None, faces1, diag1, 0.25, mask1)
    resid1 = centre(right1e - operate(field1, faces1, diag1, 0.25), HALO1)

    whole = gather_global(jnp.stack([cond2, restrict(resid1)]))
    error2 = cycle_global(whole[1], whole[0], 0.0625)

    reach = HALO1 // 2
    padded2 = jnp.pad(error2, reach)
    block2 = cond2.shape
    starts = [lax.axis_index(axis) * n for axis, n in zip(AXES, block2)]
    sizes = [n + 2 * reach for n in block2]
    error2e = lax.dynamic_slice(padded2, starts, sizes)
    field1 = jnp.where(mask1, field1 + prolong(error2e), 0.0)
    field1 = smooth(right1e, field1, faces1, diag1, 0.25, mask1)

    cut = HALO1 - HALO0 // 2
    error1e = field1[cut:-cut, cut:-cut, cut:-cut]
    field0 = jnp.where(mask0, field0 + prolong(error1e), 0.0)
    field0 = smooth(right0e, field0, faces0, diag0, 1.0, mask0)
    return centre(field0, HALO0)


def solution(mesh):
    in_specs = (P("gx", "gy", "gz"), P("gx", "gy", "gz"), P())
    out_specs = P("gx", "gy", "gz")
    return jax.shard_map(local, mesh=mesh, in_specs=in_specs, out_specs=out_specs, check_vma=False)
```

```python
import jax
import jax.numpy as jnp
from jax import lax
from jax.sharding import PartitionSpec as P

DEGREE = 3
LEVELS = 3
MATERIALS = 3

LOW = 0.3
HIGH = 2.0

AXES = ("gx", "gy", "gz")
HALO0 = 6
HALO1 = 8


def exchange(blocks, widths):
    blocks = list(blocks)
    for k, axis in enumerate(AXES):
        count = lax.axis_size(axis)
        dims = [b.ndim - 3 + k for b in blocks]
        sizes = [b.shape[d] for b, d in zip(blocks, dims)]
        reach = [-(-w // n) for w, n in zip(widths, sizes)]
        lows = [[] for _ in blocks]
        highs = [[] for _ in blocks]
        for shift in range(1, max(reach) + 1):
            users = [j for j in range(len(blocks)) if reach[j] >= shift]
            takes = {j: min(sizes[j], widths[j] - (shift - 1) * sizes[j]) for j in users}
            for side in (0, 1):
                slabs = []
                for j in users:
                    n, t = sizes[j], takes[j]
                    start = n - t if side == 0 else 0
                    slabs.append(lax.slice_in_dim(blocks[j], start, start + t, axis=dims[j]))
                if shift >= count:
                    got = [jnp.zeros_like(s) for s in slabs]
                else:
                    if side == 0:
                        pairs = [(i, i + shift) for i in range(count - shift)]
                    else:
                        pairs = [(i + shift, i) for i in range(count - shift)]
                    flat = jnp.concatenate([s.reshape(-1) for s in slabs])
                    flat = lax.ppermute(flat, axis, pairs)
                    got, at = [], 0
                    for s in slabs:
                        got.append(flat[at:at + s.size].reshape(s.shape))
                        at += s.size
                for j, g in zip(users, got):
                    (lows if side == 0 else highs)[j].append(g)
        blocks = [
            jnp.concatenate(lows[j][::-1] + [blocks[j]] + highs[j], axis=dims[j])
            for j in range(len(blocks))
        ]
    return blocks


def inside_mask(block_shape, width):
    parts = []
    for k, axis in enumerate(AXES):
        n = block_shape[k]
        total = n * lax.axis_size(axis)
        coord = lax.axis_index(axis) * n - width + jnp.arange(n + 2 * width)
        parts.append((coord >= 0) & (coord < total))
    return parts[0][:, None, None] & parts[1][None, :, None] & parts[2][None, None, :]


def harmonic(left, right):
    return 2.0 * left * right / (left + right)


def neighbours(padded):
    return (
        padded[2:, 1:-1, 1:-1],
        padded[:-2, 1:-1, 1:-1],
        padded[1:-1, 2:, 1:-1],
        padded[1:-1, :-2, 1:-1],
        padded[1:-1, 1:-1, 2:],
        padded[1:-1, 1:-1, :-2],
    )


def face_set_zero_outside(cond):
    padded = jnp.pad(cond, 1)
    faces = tuple(harmonic(cond, jnp.where(other > 0.0, other, cond)) for other in neighbours(padded))
    diag = faces[0] + faces[1] + faces[2] + faces[3] + faces[4] + faces[5]
    return faces, diag


def operate(field, faces, diag, scale):
    near = neighbours(jnp.pad(field, 1))
    total = faces[0] * near[0] + faces[1] * near[1] + faces[2] * near[2]
    total = total + faces[3] * near[3] + faces[4] * near[4] + faces[5] * near[5]
    return scale * (diag * field - total)


def smooth(right, start, faces, diag, scale, mask=None, operate=operate):
    def keep(value):
        return value if mask is None else jnp.where(mask, value, 0.0)

    theta = 0.5 * (HIGH + LOW)
    delta = 0.5 * (HIGH - LOW)
    sigma = theta / delta
    rho = 1.0 / sigma
    inverse = 1.0 / (scale * diag)
    if start is None:
        resid = right
        step_dir = inverse * resid / theta
        field = keep(step_dir)
    else:
        resid = right - operate(start, faces, diag, scale)
        step_dir = inverse * resid / theta
        field = keep(start + step_dir)
    for turn in range(DEGREE - 1):
        rho_new = 1.0 / (2.0 * sigma - rho)
        resid = right - operate(field, faces, diag, scale)
        step_dir = rho_new * rho * step_dir + 2.0 * rho_new / delta * inverse * resid
        field = keep(field + step_dir)
        rho = rho_new
    return field


def restrict(field):
    field = field[0::2] + field[1::2]
    field = field[:, 0::2] + field[:, 1::2]
    field = field[:, :, 0::2] + field[:, :, 1::2]
    return field / 8.0


def prolong(field):
    return jnp.repeat(jnp.repeat(jnp.repeat(field, 2, 0), 2, 1), 2, 2)


def centre(field, width):
    return field[width:-width, width:-width, width:-width]


def face_set_global(cond):
    padded = jnp.pad(cond, 1, mode="edge")
    faces = tuple(harmonic(cond, other) for other in neighbours(padded))
    diag = faces[0] + faces[1] + faces[2] + faces[3] + faces[4] + faces[5]
    return faces, diag


def neighbours_dilated(padded):
    return (
        padded[2:, 2:-2, 2:-2],
        padded[:-2, 2:-2, 2:-2],
        padded[1:-1, 4:, 2:-2],
        padded[1:-1, :-4, 2:-2],
        padded[1:-1, 2:-2, 4:],
        padded[1:-1, 2:-2, :-4],
    )


def face_set_dilated(cond):
    padded = jnp.concatenate([cond[:, :, :2], cond, cond[:, :, -2:]], axis=2)
    padded = jnp.concatenate([padded[:, :2], padded, padded[:, -2:]], axis=1)
    padded = jnp.pad(padded, ((1, 1), (0, 0), (0, 0)), mode="edge")
    faces = tuple(harmonic(cond, other) for other in neighbours_dilated(padded))
    diag = faces[0] + faces[1] + faces[2] + faces[3] + faces[4] + faces[5]
    return faces, diag


def operate_dilated(field, faces, diag, scale):
    near = neighbours_dilated(jnp.pad(field, ((1, 1), (2, 2), (2, 2))))
    total = faces[0] * near[0] + faces[1] * near[1] + faces[2] * near[2]
    total = total + faces[3] * near[3] + faces[4] * near[4] + faces[5] * near[5]
    return scale * (diag * field - total)


def restrict_dilated(field):
    field = field[0::2] + field[1::2]
    later = jnp.concatenate([field[:, 1:], jnp.zeros_like(field[:, :1])], axis=1)
    field = field + later
    later = jnp.concatenate([field[:, :, 1:], jnp.zeros_like(field[:, :, :1])], axis=2)
    return (field + later) / 8.0


def prolong_dilated(field):
    earlier = jnp.concatenate([jnp.zeros_like(field[:, :, :1]), field[:, :, :-1]], axis=2)
    odd = (jnp.arange(field.shape[2]) % 2 == 1)[None, None, :]
    field = jnp.where(odd, earlier, field)
    earlier = jnp.concatenate([jnp.zeros_like(field[:, :1]), field[:, :-1]], axis=1)
    odd = (jnp.arange(field.shape[1]) % 2 == 1)[None, :, None]
    field = jnp.where(odd, earlier, field)
    return jnp.repeat(field, 2, 0)


def cycle_global(right, cond, scale):
    faces, diag = face_set_global(cond)
    field = smooth(right, None, faces, diag, scale)
    resid = right - operate(field, faces, diag, scale)
    right3, cond3 = restrict_dilated(resid), restrict_dilated(cond)
    faces3, diag3 = face_set_dilated(cond3)
    scale3 = scale * 0.25
    error = smooth(right3, None, faces3, diag3, scale3, operate=operate_dilated)
    error = smooth(right3, error, faces3, diag3, scale3, operate=operate_dilated)
    field = field + prolong_dilated(error)
    return smooth(right, field, faces, diag, scale)


def gather_axis(block, axis, dim, descending=False):
    count = lax.axis_size(axis)
    if count & (count - 1):
        return lax.all_gather(block, axis, axis=dim, tiled=True)
    index = lax.axis_index(axis)
    steps = []
    step = 1
    while step < count:
        steps.append(step)
        step *= 2
    if descending:
        steps = steps[::-1]
    size = block.shape[dim]
    for step in steps:
        theirs = lax.ppermute(block, axis, [(i, i ^ step) for i in range(count)])
        upper = (index // step) % 2 == 1
        low = jnp.where(upper, theirs, block)
        high = jnp.where(upper, block, theirs)
        block = jnp.concatenate([low, high], axis=dim)
    if descending and len(steps) > 1:
        bits = len(steps)
        shape = block.shape
        split = shape[:dim] + (2,) * bits + (size,) + shape[dim + 1:]
        order = (
            list(range(dim))
            + [dim + bits - 1 - b for b in range(bits)]
            + list(range(dim + bits, len(split)))
        )
        block = block.reshape(split).transpose(order).reshape(shape)
    return block


def gather_global(block):
    block = gather_axis(block, "gz", 3)
    block = gather_axis(block, "gy", 2)
    return gather_axis(block, "gx", 1, descending=True)


def local(heat_source, material, conductivity):
    cond0 = jnp.zeros(heat_source.shape, jnp.float32)
    for which in range(MATERIALS):
        cond0 = cond0 + jnp.where(material == which, conductivity[which], jnp.float32(0.0))
    cond1 = restrict(cond0)
    cond2 = restrict(cond1)
    block0, block1 = heat_source.shape, cond1.shape

    ext0, cond1e = exchange([jnp.stack([cond0, heat_source]), cond1], [HALO0, HALO1])
    cond0e, right0e = ext0[0], ext0[1]

    mask0 = inside_mask(block0, HALO0)
    faces0, diag0 = face_set_zero_outside(cond0e)
    field0 = smooth(right0e, None, faces0, diag0, 1.0, mask0)
    resid0 = centre(right0e - operate(field0, faces0, diag0, 1.0), HALO0)

    faces1, diag1 = face_set_zero_outside(cond1e)
    mask1 = inside_mask(block1, HALO1)
    (right1e,) = exchange([restrict(resid0)], [HALO1])
    field1 = smooth(right1e, None, faces1, diag1, 0.25, mask1)
    resid1 = centre(right1e - operate(field1, faces1, diag1, 0.25), HALO1)

    whole = gather_global(jnp.stack([cond2, restrict(resid1)]))
    error2 = cycle_global(whole[1], whole[0], 0.0625)

    reach = HALO1 // 2
    padded2 = jnp.pad(error2, reach)
    block2 = cond2.shape
    starts = [lax.axis_index(axis) * n for axis, n in zip(AXES, block2)]
    sizes = [n + 2 * reach for n in block2]
    error2e = lax.dynamic_slice(padded2, starts, sizes)
    field1 = jnp.where(mask1, field1 + prolong(error2e), 0.0)
    field1 = smooth(right1e, field1, faces1, diag1, 0.25, mask1)

    cut = HALO1 - HALO0 // 2
    error1e = field1[cut:-cut, cut:-cut, cut:-cut]
    field0 = jnp.where(mask0, field0 + prolong(error1e), 0.0)
    field0 = smooth(right0e, field0, faces0, diag0, 1.0, mask0)
    return centre(field0, HALO0)


def solution(mesh):
    in_specs = (P("gx", "gy", "gz"), P("gx", "gy", "gz"), P())
    out_specs = P("gx", "gy", "gz")
    return jax.shard_map(local, mesh=mesh, in_specs=in_specs, out_specs=out_specs, check_vma=False)
```

```python
import jax
import jax.numpy as jnp
from jax import lax
from jax.sharding import PartitionSpec as P

DEGREE = 3
LEVELS = 3
MATERIALS = 3

LOW = 0.3
HIGH = 2.0

AXES = ("gx", "gy", "gz")
ROUND_ORDER = (1, 2, 0)
HALO0 = 6
HALO1 = 8


def exchange(blocks, widths):
    blocks = list(blocks)
    for k in ROUND_ORDER:
        axis = AXES[k]
        count = lax.axis_size(axis)
        dims = [b.ndim - 3 + k for b in blocks]
        sizes = [b.shape[d] for b, d in zip(blocks, dims)]
        reach = [-(-w // n) for w, n in zip(widths, sizes)]
        lows = [[] for _ in blocks]
        highs = [[] for _ in blocks]
        for shift in range(1, max(reach) + 1):
            users = [j for j in range(len(blocks)) if reach[j] >= shift]
            takes = {j: min(sizes[j], widths[j] - (shift - 1) * sizes[j]) for j in users}
            for side in (0, 1):
                slabs = []
                for j in users:
                    n, t = sizes[j], takes[j]
                    start = n - t if side == 0 else 0
                    slabs.append(lax.slice_in_dim(blocks[j], start, start + t, axis=dims[j]))
                if shift >= count:
                    got = [jnp.zeros_like(s) for s in slabs]
                else:
                    if side == 0:
                        pairs = [(i, i + shift) for i in range(count - shift)]
                    else:
                        pairs = [(i + shift, i) for i in range(count - shift)]
                    flat = jnp.concatenate([s.reshape(-1) for s in slabs])
                    flat = lax.ppermute(flat, axis, pairs)
                    got, at = [], 0
                    for s in slabs:
                        got.append(flat[at:at + s.size].reshape(s.shape))
                        at += s.size
                for j, g in zip(users, got):
                    (lows if side == 0 else highs)[j].append(g)
        blocks = [
            jnp.concatenate(lows[j][::-1] + [blocks[j]] + highs[j], axis=dims[j])
            for j in range(len(blocks))
        ]
    return blocks


def inside_mask(block_shape, width):
    parts = []
    for k, axis in enumerate(AXES):
        n = block_shape[k]
        total = n * lax.axis_size(axis)
        coord = lax.axis_index(axis) * n - width + jnp.arange(n + 2 * width)
        parts.append((coord >= 0) & (coord < total))
    return parts[0][:, None, None] & parts[1][None, :, None] & parts[2][None, None, :]


def harmonic(left, right):
    return 2.0 * left * right / (left + right)


def neighbours(padded):
    return (
        padded[2:, 1:-1, 1:-1],
        padded[:-2, 1:-1, 1:-1],
        padded[1:-1, 2:, 1:-1],
        padded[1:-1, :-2, 1:-1],
        padded[1:-1, 1:-1, 2:],
        padded[1:-1, 1:-1, :-2],
    )


def face_set_zero_outside(cond):
    padded = jnp.pad(cond, 1)
    faces = tuple(harmonic(cond, jnp.where(other > 0.0, other, cond)) for other in neighbours(padded))
    diag = faces[0] + faces[1] + faces[2] + faces[3] + faces[4] + faces[5]
    return faces, diag


def operate(field, faces, diag, scale):
    near = neighbours(jnp.pad(field, 1))
    total = faces[0] * near[0] + faces[1] * near[1] + faces[2] * near[2]
    total = total + faces[3] * near[3] + faces[4] * near[4] + faces[5] * near[5]
    return scale * (diag * field - total)


def smooth(right, start, faces, diag, scale, mask=None, operate=operate):
    def keep(value):
        return value if mask is None else jnp.where(mask, value, 0.0)

    theta = 0.5 * (HIGH + LOW)
    delta = 0.5 * (HIGH - LOW)
    sigma = theta / delta
    rho = 1.0 / sigma
    inverse = 1.0 / (scale * diag)
    if start is None:
        resid = right
        step_dir = inverse * resid / theta
        field = keep(step_dir)
    else:
        resid = right - operate(start, faces, diag, scale)
        step_dir = inverse * resid / theta
        field = keep(start + step_dir)
    for turn in range(DEGREE - 1):
        rho_new = 1.0 / (2.0 * sigma - rho)
        resid = right - operate(field, faces, diag, scale)
        step_dir = rho_new * rho * step_dir + 2.0 * rho_new / delta * inverse * resid
        field = keep(field + step_dir)
        rho = rho_new
    return field


def restrict(field):
    field = field[0::2] + field[1::2]
    field = field[:, 0::2] + field[:, 1::2]
    field = field[:, :, 0::2] + field[:, :, 1::2]
    return field / 8.0


def prolong(field):
    return jnp.repeat(jnp.repeat(jnp.repeat(field, 2, 0), 2, 1), 2, 2)


def centre(field, width):
    return field[width:-width, width:-width, width:-width]


def face_set_global(cond):
    padded = jnp.pad(cond, 1, mode="edge")
    faces = tuple(harmonic(cond, other) for other in neighbours(padded))
    diag = faces[0] + faces[1] + faces[2] + faces[3] + faces[4] + faces[5]
    return faces, diag


def neighbours_dilated(padded):
    return (
        padded[2:, 1:-1, 2:-2],
        padded[:-2, 1:-1, 2:-2],
        padded[1:-1, 2:, 2:-2],
        padded[1:-1, :-2, 2:-2],
        padded[1:-1, 1:-1, 4:],
        padded[1:-1, 1:-1, :-4],
    )


def face_set_dilated(cond):
    padded = jnp.concatenate([cond[:, :, :2], cond, cond[:, :, -2:]], axis=2)
    padded = jnp.pad(padded, ((1, 1), (1, 1), (0, 0)), mode="edge")
    faces = tuple(harmonic(cond, other) for other in neighbours_dilated(padded))
    diag = faces[0] + faces[1] + faces[2] + faces[3] + faces[4] + faces[5]
    return faces, diag


def operate_dilated(field, faces, diag, scale):
    near = neighbours_dilated(jnp.pad(field, ((1, 1), (1, 1), (2, 2))))
    total = faces[0] * near[0] + faces[1] * near[1] + faces[2] * near[2]
    total = total + faces[3] * near[3] + faces[4] * near[4] + faces[5] * near[5]
    return scale * (diag * field - total)


def restrict_dilated(field):
    field = field[0::2] + field[1::2]
    field = field[:, 0::2] + field[:, 1::2]
    later = jnp.concatenate([field[:, :, 1:], jnp.zeros_like(field[:, :, :1])], axis=2)
    return (field + later) / 8.0


def prolong_dilated(field):
    earlier = jnp.concatenate([jnp.zeros_like(field[:, :, :1]), field[:, :, :-1]], axis=2)
    odd = (jnp.arange(field.shape[2]) % 2 == 1)[None, None, :]
    field = jnp.where(odd, earlier, field)
    return jnp.repeat(jnp.repeat(field, 2, 0), 2, 1)


def cycle_global(right, cond, scale):
    faces, diag = face_set_global(cond)
    field = smooth(right, None, faces, diag, scale)
    resid = right - operate(field, faces, diag, scale)
    right3, cond3 = restrict_dilated(resid), restrict_dilated(cond)
    faces3, diag3 = face_set_dilated(cond3)
    scale3 = scale * 0.25
    error = smooth(right3, None, faces3, diag3, scale3, operate=operate_dilated)
    error = smooth(right3, error, faces3, diag3, scale3, operate=operate_dilated)
    field = field + prolong_dilated(error)
    return smooth(right, field, faces, diag, scale)


def gather_axis(block, axis, dim, descending=False):
    count = lax.axis_size(axis)
    if count & (count - 1):
        return lax.all_gather(block, axis, axis=dim, tiled=True)
    index = lax.axis_index(axis)
    steps = []
    step = 1
    while step < count:
        steps.append(step)
        step *= 2
    if descending:
        steps = steps[::-1]
    size = block.shape[dim]
    for step in steps:
        theirs = lax.ppermute(block, axis, [(i, i ^ step) for i in range(count)])
        upper = (index // step) % 2 == 1
        low = jnp.where(upper, theirs, block)
        high = jnp.where(upper, block, theirs)
        block = jnp.concatenate([low, high], axis=dim)
    if descending and len(steps) > 1:
        bits = len(steps)
        shape = block.shape
        split = shape[:dim] + (2,) * bits + (size,) + shape[dim + 1:]
        order = (
            list(range(dim))
            + [dim + bits - 1 - b for b in range(bits)]
            + list(range(dim + bits, len(split)))
        )
        block = block.reshape(split).transpose(order).reshape(shape)
    return block


def gather_global(block):
    block = gather_axis(block, "gz", 3)
    block = gather_axis(block, "gy", 2)
    return gather_axis(block, "gx", 1, descending=True)


def local(heat_source, material, conductivity):
    cond0 = jnp.zeros(heat_source.shape, jnp.float32)
    for which in range(MATERIALS):
        cond0 = cond0 + jnp.where(material == which, conductivity[which], jnp.float32(0.0))
    cond1 = restrict(cond0)
    cond2 = restrict(cond1)
    block0, block1 = heat_source.shape, cond1.shape

    ext0, cond1e = exchange([jnp.stack([cond0, heat_source]), cond1], [HALO0, HALO1])
    cond0e, right0e = ext0[0], ext0[1]

    mask0 = inside_mask(block0, HALO0)
    faces0, diag0 = face_set_zero_outside(cond0e)
    field0 = smooth(right0e, None, faces0, diag0, 1.0, mask0)
    resid0 = centre(right0e - operate(field0, faces0, diag0, 1.0), HALO0)

    faces1, diag1 = face_set_zero_outside(cond1e)
    mask1 = inside_mask(block1, HALO1)
    (right1e,) = exchange([restrict(resid0)], [HALO1])
    field1 = smooth(right1e, None, faces1, diag1, 0.25, mask1)
    resid1 = centre(right1e - operate(field1, faces1, diag1, 0.25), HALO1)

    whole = gather_global(jnp.stack([cond2, restrict(resid1)]))
    error2 = cycle_global(whole[1], whole[0], 0.0625)

    reach = HALO1 // 2
    padded2 = jnp.pad(error2, reach)
    block2 = cond2.shape
    starts = [lax.axis_index(axis) * n for axis, n in zip(AXES, block2)]
    sizes = [n + 2 * reach for n in block2]
    error2e = lax.dynamic_slice(padded2, starts, sizes)
    field1 = jnp.where(mask1, field1 + prolong(error2e), 0.0)
    field1 = smooth(right1e, field1, faces1, diag1, 0.25, mask1)

    cut = HALO1 - HALO0 // 2
    error1e = field1[cut:-cut, cut:-cut, cut:-cut]
    field0 = jnp.where(mask0, field0 + prolong(error1e), 0.0)
    field0 = smooth(right0e, field0, faces0, diag0, 1.0, mask0)
    return centre(field0, HALO0)


def solution(mesh):
    in_specs = (P("gx", "gy", "gz"), P("gx", "gy", "gz"), P())
    out_specs = P("gx", "gy", "gz")
    return jax.shard_map(local, mesh=mesh, in_specs=in_specs, out_specs=out_specs, check_vma=False)
```

```python
import jax
import jax.numpy as jnp
from jax import lax
from jax.sharding import PartitionSpec as P

DEGREE = 3
LEVELS = 3
MATERIALS = 3

LOW = 0.3
HIGH = 2.0

AXES = ("gx", "gy", "gz")
HALO0 = 6
HALO1 = 8


def exchange(blocks, widths):
    blocks = list(blocks)
    for k, axis in enumerate(AXES):
        count = lax.axis_size(axis)
        dims = [b.ndim - 3 + k for b in blocks]
        sizes = [b.shape[d] for b, d in zip(blocks, dims)]
        reach = [-(-w // n) for w, n in zip(widths, sizes)]
        lows = [[] for _ in blocks]
        highs = [[] for _ in blocks]
        for shift in range(1, max(reach) + 1):
            users = [j for j in range(len(blocks)) if reach[j] >= shift]
            takes = {j: min(sizes[j], widths[j] - (shift - 1) * sizes[j]) for j in users}
            for side in (0, 1):
                slabs = []
                for j in users:
                    n, t = sizes[j], takes[j]
                    start = n - t if side == 0 else 0
                    slabs.append(lax.slice_in_dim(blocks[j], start, start + t, axis=dims[j]))
                if shift >= count:
                    got = [jnp.zeros_like(s) for s in slabs]
                else:
                    if side == 0:
                        pairs = [(i, i + shift) for i in range(count - shift)]
                    else:
                        pairs = [(i + shift, i) for i in range(count - shift)]
                    flat = jnp.concatenate([s.reshape(-1) for s in slabs])
                    flat = lax.ppermute(flat, axis, pairs)
                    got, at = [], 0
                    for s in slabs:
                        got.append(flat[at:at + s.size].reshape(s.shape))
                        at += s.size
                for j, g in zip(users, got):
                    (lows if side == 0 else highs)[j].append(g)
        blocks = [
            jnp.concatenate(lows[j][::-1] + [blocks[j]] + highs[j], axis=dims[j])
            for j in range(len(blocks))
        ]
    return blocks


def inside_mask(block_shape, width):
    parts = []
    for k, axis in enumerate(AXES):
        n = block_shape[k]
        total = n * lax.axis_size(axis)
        coord = lax.axis_index(axis) * n - width + jnp.arange(n + 2 * width)
        parts.append((coord >= 0) & (coord < total))
    return parts[0][:, None, None] & parts[1][None, :, None] & parts[2][None, None, :]


def harmonic(left, right):
    return 2.0 * left * right / (left + right)


def neighbours(padded):
    return (
        padded[2:, 1:-1, 1:-1],
        padded[:-2, 1:-1, 1:-1],
        padded[1:-1, 2:, 1:-1],
        padded[1:-1, :-2, 1:-1],
        padded[1:-1, 1:-1, 2:],
        padded[1:-1, 1:-1, :-2],
    )


def face_set_zero_outside(cond):
    padded = jnp.pad(cond, 1)
    faces = tuple(harmonic(cond, jnp.where(other > 0.0, other, cond)) for other in neighbours(padded))
    diag = faces[0] + faces[1] + faces[2] + faces[3] + faces[4] + faces[5]
    return faces, diag


def operate(field, faces, diag, scale):
    near = neighbours(jnp.pad(field, 1))
    total = faces[0] * near[0] + faces[1] * near[1] + faces[2] * near[2]
    total = total + faces[3] * near[3] + faces[4] * near[4] + faces[5] * near[5]
    return scale * (diag * field - total)


def smooth(right, start, faces, diag, scale, mask=None, operate=operate):
    def keep(value):
        return value if mask is None else jnp.where(mask, value, 0.0)

    theta = 0.5 * (HIGH + LOW)
    delta = 0.5 * (HIGH - LOW)
    sigma = theta / delta
    rho = 1.0 / sigma
    inverse = 1.0 / (scale * diag)
    if start is None:
        resid = right
        step_dir = inverse * resid / theta
        field = keep(step_dir)
    else:
        resid = right - operate(start, faces, diag, scale)
        step_dir = inverse * resid / theta
        field = keep(start + step_dir)
    for turn in range(DEGREE - 1):
        rho_new = 1.0 / (2.0 * sigma - rho)
        resid = right - operate(field, faces, diag, scale)
        step_dir = rho_new * rho * step_dir + 2.0 * rho_new / delta * inverse * resid
        field = keep(field + step_dir)
        rho = rho_new
    return field


def smooth_shrinking(right, start, faces, diag, scale, mask, full, valid):
    def at(value, width):
        cut = full - width
        return value if cut == 0 else value[cut:-cut, cut:-cut, cut:-cut]

    def apply(field, width):
        near = neighbours(field)
        fs = [at(f, width) for f in faces]
        total = fs[0] * near[0] + fs[1] * near[1] + fs[2] * near[2]
        total = total + fs[3] * near[3] + fs[4] * near[4] + fs[5] * near[5]
        return scale * (at(diag, width) * centre(field, 1) - total)

    theta = 0.5 * (HIGH + LOW)
    delta = 0.5 * (HIGH - LOW)
    sigma = theta / delta
    rho = 1.0 / sigma
    inverse = 1.0 / (scale * diag)
    width = valid - 1
    field = at(start, valid)
    resid = at(right, width) - apply(field, width)
    step_dir = at(inverse, width) * resid / theta
    field = jnp.where(at(mask, width), centre(field, 1) + step_dir, 0.0)
    for turn in range(DEGREE - 1):
        rho_new = 1.0 / (2.0 * sigma - rho)
        width -= 1
        resid = at(right, width) - apply(field, width)
        step_dir = rho_new * rho * centre(step_dir, 1) + 2.0 * rho_new / delta * at(inverse, width) * resid
        field = jnp.where(at(mask, width), centre(field, 1) + step_dir, 0.0)
        rho = rho_new
    return field


def restrict(field):
    field = field[0::2] + field[1::2]
    field = field[:, 0::2] + field[:, 1::2]
    field = field[:, :, 0::2] + field[:, :, 1::2]
    return field / 8.0


def prolong(field):
    return jnp.repeat(jnp.repeat(jnp.repeat(field, 2, 0), 2, 1), 2, 2)


def centre(field, width):
    return field[width:-width, width:-width, width:-width]


def face_set_global(cond):
    padded = jnp.pad(cond, 1, mode="edge")
    faces = tuple(harmonic(cond, other) for other in neighbours(padded))
    diag = faces[0] + faces[1] + faces[2] + faces[3] + faces[4] + faces[5]
    return faces, diag


def neighbours_dilated(padded):
    return (
        padded[2:, 1:-1, 2:-2],
        padded[:-2, 1:-1, 2:-2],
        padded[1:-1, 2:, 2:-2],
        padded[1:-1, :-2, 2:-2],
        padded[1:-1, 1:-1, 4:],
        padded[1:-1, 1:-1, :-4],
    )


def face_set_dilated(cond):
    padded = jnp.concatenate([cond[:, :, :2], cond, cond[:, :, -2:]], axis=2)
    padded = jnp.pad(padded, ((1, 1), (1, 1), (0, 0)), mode="edge")
    faces = tuple(harmonic(cond, other) for other in neighbours_dilated(padded))
    diag = faces[0] + faces[1] + faces[2] + faces[3] + faces[4] + faces[5]
    return faces, diag


def operate_dilated(field, faces, diag, scale):
    near = neighbours_dilated(jnp.pad(field, ((1, 1), (1, 1), (2, 2))))
    total = faces[0] * near[0] + faces[1] * near[1] + faces[2] * near[2]
    total = total + faces[3] * near[3] + faces[4] * near[4] + faces[5] * near[5]
    return scale * (diag * field - total)


def restrict_dilated(field):
    field = field[0::2] + field[1::2]
    field = field[:, 0::2] + field[:, 1::2]
    later = jnp.concatenate([field[:, :, 1:], jnp.zeros_like(field[:, :, :1])], axis=2)
    return (field + later) / 8.0


def prolong_dilated(field):
    earlier = jnp.concatenate([jnp.zeros_like(field[:, :, :1]), field[:, :, :-1]], axis=2)
    odd = (jnp.arange(field.shape[2]) % 2 == 1)[None, None, :]
    field = jnp.where(odd, earlier, field)
    return jnp.repeat(jnp.repeat(field, 2, 0), 2, 1)


def cycle_global(right, cond, scale):
    faces, diag = face_set_global(cond)
    field = smooth(right, None, faces, diag, scale)
    resid = right - operate(field, faces, diag, scale)
    right3, cond3 = restrict_dilated(resid), restrict_dilated(cond)
    faces3, diag3 = face_set_dilated(cond3)
    scale3 = scale * 0.25
    error = smooth(right3, None, faces3, diag3, scale3, operate=operate_dilated)
    error = smooth(right3, error, faces3, diag3, scale3, operate=operate_dilated)
    field = field + prolong_dilated(error)
    return smooth(right, field, faces, diag, scale)


def gather_axis(block, axis, dim, descending=False):
    count = lax.axis_size(axis)
    if count & (count - 1):
        return lax.all_gather(block, axis, axis=dim, tiled=True)
    index = lax.axis_index(axis)
    steps = []
    step = 1
    while step < count:
        steps.append(step)
        step *= 2
    if descending:
        steps = steps[::-1]
    size = block.shape[dim]
    for step in steps:
        theirs = lax.ppermute(block, axis, [(i, i ^ step) for i in range(count)])
        upper = (index // step) % 2 == 1
        low = jnp.where(upper, theirs, block)
        high = jnp.where(upper, block, theirs)
        block = jnp.concatenate([low, high], axis=dim)
    if descending and len(steps) > 1:
        bits = len(steps)
        shape = block.shape
        split = shape[:dim] + (2,) * bits + (size,) + shape[dim + 1:]
        order = (
            list(range(dim))
            + [dim + bits - 1 - b for b in range(bits)]
            + list(range(dim + bits, len(split)))
        )
        block = block.reshape(split).transpose(order).reshape(shape)
    return block


def gather_global(block):
    block = gather_axis(block, "gz", 3)
    block = gather_axis(block, "gy", 2)
    return gather_axis(block, "gx", 1, descending=True)


def local(heat_source, material, conductivity):
    cond0 = jnp.zeros(heat_source.shape, jnp.float32)
    for which in range(MATERIALS):
        cond0 = cond0 + jnp.where(material == which, conductivity[which], jnp.float32(0.0))
    cond1 = restrict(cond0)
    cond2 = restrict(cond1)
    block0, block1 = heat_source.shape, cond1.shape

    ext0, cond1e = exchange([jnp.stack([cond0, heat_source]), cond1], [HALO0, HALO1])
    cond0e, right0e = ext0[0], ext0[1]

    mask0 = inside_mask(block0, HALO0)
    faces0, diag0 = face_set_zero_outside(cond0e)
    field0 = smooth(right0e, None, faces0, diag0, 1.0, mask0)
    resid0 = centre(right0e - operate(field0, faces0, diag0, 1.0), HALO0)

    faces1, diag1 = face_set_zero_outside(cond1e)
    mask1 = inside_mask(block1, HALO1)
    (right1e,) = exchange([restrict(resid0)], [HALO1])
    field1 = smooth(right1e, None, faces1, diag1, 0.25, mask1)
    resid1 = centre(right1e - operate(field1, faces1, diag1, 0.25), HALO1)

    whole = gather_global(jnp.stack([cond2, restrict(resid1)]))
    error2 = cycle_global(whole[1], whole[0], 0.0625)

    reach = HALO1 // 2
    padded2 = jnp.pad(error2, reach)
    block2 = cond2.shape
    starts = [lax.axis_index(axis) * n for axis, n in zip(AXES, block2)]
    sizes = [n + 2 * reach for n in block2]
    error2e = lax.dynamic_slice(padded2, starts, sizes)
    field1 = jnp.where(mask1, field1 + prolong(error2e), 0.0)
    field1 = smooth_shrinking(right1e, field1, faces1, diag1, 0.25, mask1, HALO1, HALO1 - 3)

    error1e = jnp.pad(field1, HALO0 // 2 - (HALO1 - 6))
    field0 = jnp.where(mask0, field0 + prolong(error1e), 0.0)
    return smooth_shrinking(right0e, field0, faces0, diag0, 1.0, mask0, HALO0, 3)


def solution(mesh):
    in_specs = (P("gx", "gy", "gz"), P("gx", "gy", "gz"), P())
    out_specs = P("gx", "gy", "gz")
    return jax.shard_map(local, mesh=mesh, in_specs=in_specs, out_specs=out_specs, check_vma=False)
```

```python
import jax
import jax.numpy as jnp
from jax import lax
from jax.sharding import PartitionSpec as P

DEGREE = 3
LEVELS = 3
MATERIALS = 3

LOW = 0.3
HIGH = 2.0

AXES = ("gx", "gy", "gz")
HALO0 = 6
HALO1 = 8


def exchange(blocks, widths):
    blocks = list(blocks)
    for k, axis in enumerate(AXES):
        count = lax.axis_size(axis)
        dims = [b.ndim - 3 + k for b in blocks]
        sizes = [b.shape[d] for b, d in zip(blocks, dims)]
        reach = [-(-w // n) for w, n in zip(widths, sizes)]
        lows = [[] for _ in blocks]
        highs = [[] for _ in blocks]
        for shift in range(1, max(reach) + 1):
            users = [j for j in range(len(blocks)) if reach[j] >= shift]
            takes = {j: min(sizes[j], widths[j] - (shift - 1) * sizes[j]) for j in users}
            for side in (0, 1):
                slabs = []
                for j in users:
                    n, t = sizes[j], takes[j]
                    start = n - t if side == 0 else 0
                    slabs.append(lax.slice_in_dim(blocks[j], start, start + t, axis=dims[j]))
                if shift >= count:
                    got = [jnp.zeros_like(s) for s in slabs]
                else:
                    if side == 0:
                        pairs = [(i, i + shift) for i in range(count - shift)]
                    else:
                        pairs = [(i + shift, i) for i in range(count - shift)]
                    flat = jnp.concatenate([s.reshape(-1) for s in slabs])
                    flat = lax.ppermute(flat, axis, pairs)
                    got, at = [], 0
                    for s in slabs:
                        got.append(flat[at:at + s.size].reshape(s.shape))
                        at += s.size
                for j, g in zip(users, got):
                    (lows if side == 0 else highs)[j].append(g)
        blocks = [
            jnp.concatenate(lows[j][::-1] + [blocks[j]] + highs[j], axis=dims[j])
            for j in range(len(blocks))
        ]
    return blocks


def inside_mask(block_shape, width):
    parts = []
    for k, axis in enumerate(AXES):
        n = block_shape[k]
        total = n * lax.axis_size(axis)
        coord = lax.axis_index(axis) * n - width + jnp.arange(n + 2 * width)
        parts.append((coord >= 0) & (coord < total))
    return parts[0][:, None, None] & parts[1][None, :, None] & parts[2][None, None, :]


def harmonic(left, right):
    return 2.0 * left * right / (left + right)


def neighbours(padded):
    return (
        padded[2:, 1:-1, 1:-1],
        padded[:-2, 1:-1, 1:-1],
        padded[1:-1, 2:, 1:-1],
        padded[1:-1, :-2, 1:-1],
        padded[1:-1, 1:-1, 2:],
        padded[1:-1, 1:-1, :-2],
    )


def face_set_zero_outside(cond):
    padded = jnp.pad(cond, 1)
    faces = tuple(harmonic(cond, jnp.where(other > 0.0, other, cond)) for other in neighbours(padded))
    diag = faces[0] + faces[1] + faces[2] + faces[3] + faces[4] + faces[5]
    return faces, diag


def operate(field, faces, diag, scale):
    near = neighbours(jnp.pad(field, 1))
    total = faces[0] * near[0] + faces[1] * near[1] + faces[2] * near[2]
    total = total + faces[3] * near[3] + faces[4] * near[4] + faces[5] * near[5]
    return scale * (diag * field - total)


def smooth(right, start, faces, diag, scale, mask=None, operate=operate):
    def keep(value):
        return value if mask is None else jnp.where(mask, value, 0.0)

    theta = 0.5 * (HIGH + LOW)
    delta = 0.5 * (HIGH - LOW)
    sigma = theta / delta
    rho = 1.0 / sigma
    inverse = 1.0 / (scale * diag)
    if start is None:
        resid = right
        step_dir = inverse * resid / theta
        field = keep(step_dir)
    else:
        resid = right - operate(start, faces, diag, scale)
        step_dir = inverse * resid / theta
        field = keep(start + step_dir)
    for turn in range(DEGREE - 1):
        rho_new = 1.0 / (2.0 * sigma - rho)
        resid = right - operate(field, faces, diag, scale)
        step_dir = rho_new * rho * step_dir + 2.0 * rho_new / delta * inverse * resid
        field = keep(field + step_dir)
        rho = rho_new
    return field


def restrict(field):
    field = field[0::2] + field[1::2]
    field = field[:, 0::2] + field[:, 1::2]
    field = field[:, :, 0::2] + field[:, :, 1::2]
    return field / 8.0


def prolong(field):
    return jnp.repeat(jnp.repeat(jnp.repeat(field, 2, 0), 2, 1), 2, 2)


def centre(field, width):
    return field[width:-width, width:-width, width:-width]


def face_set_global(cond):
    padded = jnp.pad(cond, 1, mode="edge")
    faces = tuple(harmonic(cond, other) for other in neighbours(padded))
    diag = faces[0] + faces[1] + faces[2] + faces[3] + faces[4] + faces[5]
    return faces, diag


def neighbours_dilated(padded):
    return (
        padded[2:, 1:-1, 2:-2],
        padded[:-2, 1:-1, 2:-2],
        padded[1:-1, 2:, 2:-2],
        padded[1:-1, :-2, 2:-2],
        padded[1:-1, 1:-1, 4:],
        padded[1:-1, 1:-1, :-4],
    )


def face_set_dilated(cond):
    padded = jnp.concatenate([cond[:, :, :2], cond, cond[:, :, -2:]], axis=2)
    padded = jnp.pad(padded, ((1, 1), (1, 1), (0, 0)), mode="edge")
    faces = tuple(harmonic(cond, other) for other in neighbours_dilated(padded))
    diag = faces[0] + faces[1] + faces[2] + faces[3] + faces[4] + faces[5]
    return faces, diag


def operate_dilated(field, faces, diag, scale):
    near = neighbours_dilated(jnp.pad(field, ((1, 1), (1, 1), (2, 2))))
    total = faces[0] * near[0] + faces[1] * near[1] + faces[2] * near[2]
    total = total + faces[3] * near[3] + faces[4] * near[4] + faces[5] * near[5]
    return scale * (diag * field - total)


def restrict_dilated(field):
    field = field[0::2] + field[1::2]
    field = field[:, 0::2] + field[:, 1::2]
    later = jnp.concatenate([field[:, :, 1:], jnp.zeros_like(field[:, :, :1])], axis=2)
    return (field + later) / 8.0


def prolong_dilated(field):
    earlier = jnp.concatenate([jnp.zeros_like(field[:, :, :1]), field[:, :, :-1]], axis=2)
    odd = (jnp.arange(field.shape[2]) % 2 == 1)[None, None, :]
    field = jnp.where(odd, earlier, field)
    return jnp.repeat(jnp.repeat(field, 2, 0), 2, 1)


def cycle_global(right, cond, scale):
    faces, diag = face_set_global(cond)
    field = smooth(right, None, faces, diag, scale)
    resid = right - operate(field, faces, diag, scale)
    right3, cond3 = restrict_dilated(resid), restrict_dilated(cond)
    faces3, diag3 = face_set_dilated(cond3)
    scale3 = scale * 0.25
    error = smooth(right3, None, faces3, diag3, scale3, operate=operate_dilated)
    error = smooth(right3, error, faces3, diag3, scale3, operate=operate_dilated)
    field = field + prolong_dilated(error)
    return smooth(right, field, faces, diag, scale)


def gather_axis(block, axis, dim, descending=False):
    count = lax.axis_size(axis)
    if count & (count - 1):
        return lax.all_gather(block, axis, axis=dim, tiled=True)
    index = lax.axis_index(axis)
    steps = []
    step = 1
    while step < count:
        steps.append(step)
        step *= 2
    if descending:
        steps = steps[::-1]
    size = block.shape[dim]
    for step in steps:
        theirs = lax.ppermute(block, axis, [(i, i ^ step) for i in range(count)])
        upper = (index // step) % 2 == 1
        low = jnp.where(upper, theirs, block)
        high = jnp.where(upper, block, theirs)
        block = jnp.concatenate([low, high], axis=dim)
    if descending and len(steps) > 1:
        bits = len(steps)
        shape = block.shape
        split = shape[:dim] + (2,) * bits + (size,) + shape[dim + 1:]
        order = (
            list(range(dim))
            + [dim + bits - 1 - b for b in range(bits)]
            + list(range(dim + bits, len(split)))
        )
        block = block.reshape(split).transpose(order).reshape(shape)
    return block


def gather_global(block):
    block = gather_axis(block, "gy", 2)
    block = gather_axis(block, "gz", 3)
    return gather_axis(block, "gx", 1, descending=True)


def local(heat_source, material, conductivity):
    cond0 = jnp.zeros(heat_source.shape, jnp.float32)
    for which in range(MATERIALS):
        cond0 = cond0 + jnp.where(material == which, conductivity[which], jnp.float32(0.0))
    cond1 = restrict(cond0)
    cond2 = restrict(cond1)
    block0, block1 = heat_source.shape, cond1.shape

    ext0, cond1e = exchange([jnp.stack([cond0, heat_source]), cond1], [HALO0, HALO1])
    cond0e, right0e = ext0[0], ext0[1]

    mask0 = inside_mask(block0, HALO0)
    faces0, diag0 = face_set_zero_outside(cond0e)
    field0 = smooth(right0e, None, faces0, diag0, 1.0, mask0)
    resid0 = centre(right0e - operate(field0, faces0, diag0, 1.0), HALO0)

    faces1, diag1 = face_set_zero_outside(cond1e)
    mask1 = inside_mask(block1, HALO1)
    (right1e,) = exchange([restrict(resid0)], [HALO1])
    field1 = smooth(right1e, None, faces1, diag1, 0.25, mask1)
    resid1 = centre(right1e - operate(field1, faces1, diag1, 0.25), HALO1)

    whole = gather_global(jnp.stack([cond2, restrict(resid1)]))
    error2 = cycle_global(whole[1], whole[0], 0.0625)

    reach = HALO1 // 2
    padded2 = jnp.pad(error2, reach)
    block2 = cond2.shape
    starts = [lax.axis_index(axis) * n for axis, n in zip(AXES, block2)]
    sizes = [n + 2 * reach for n in block2]
    error2e = lax.dynamic_slice(padded2, starts, sizes)
    field1 = jnp.where(mask1, field1 + prolong(error2e), 0.0)
    field1 = smooth(right1e, field1, faces1, diag1, 0.25, mask1)

    cut = HALO1 - HALO0 // 2
    error1e = field1[cut:-cut, cut:-cut, cut:-cut]
    field0 = jnp.where(mask0, field0 + prolong(error1e), 0.0)
    field0 = smooth(right0e, field0, faces0, diag0, 1.0, mask0)
    return centre(field0, HALO0)


def solution(mesh):
    in_specs = (P("gx", "gy", "gz"), P("gx", "gy", "gz"), P())
    out_specs = P("gx", "gy", "gz")
    return jax.shard_map(local, mesh=mesh, in_specs=in_specs, out_specs=out_specs, check_vma=False)
```

```python
import jax
import jax.numpy as jnp
from jax import lax
from jax.sharding import PartitionSpec as P

DEGREE = 3
LEVELS = 3
MATERIALS = 3

LOW = 0.3
HIGH = 2.0

AXES = ("gx", "gy", "gz")
HALO0 = 6
HALO1 = 8


def exchange(blocks, widths):
    blocks = list(blocks)
    for k, axis in enumerate(AXES):
        count = lax.axis_size(axis)
        dims = [b.ndim - 3 + k for b in blocks]
        sizes = [b.shape[d] for b, d in zip(blocks, dims)]
        reach = [-(-w // n) for w, n in zip(widths, sizes)]
        lows = [[] for _ in blocks]
        highs = [[] for _ in blocks]
        for shift in range(1, max(reach) + 1):
            users = [j for j in range(len(blocks)) if reach[j] >= shift]
            takes = {j: min(sizes[j], widths[j] - (shift - 1) * sizes[j]) for j in users}
            for side in (0, 1):
                slabs = []
                for j in users:
                    n, t = sizes[j], takes[j]
                    start = n - t if side == 0 else 0
                    slabs.append(lax.slice_in_dim(blocks[j], start, start + t, axis=dims[j]))
                if shift >= count:
                    got = [jnp.zeros_like(s) for s in slabs]
                else:
                    if side == 0:
                        pairs = [(i, i + shift) for i in range(count - shift)]
                    else:
                        pairs = [(i + shift, i) for i in range(count - shift)]
                    if len(slabs) == 1:
                        got = [lax.ppermute(slabs[0], axis, pairs)]
                    else:
                        flat = jnp.concatenate([s.reshape(-1) for s in slabs])
                        flat = lax.ppermute(flat, axis, pairs)
                        got, at = [], 0
                        for s in slabs:
                            got.append(flat[at:at + s.size].reshape(s.shape))
                            at += s.size
                for j, g in zip(users, got):
                    (lows if side == 0 else highs)[j].append(g)
        blocks = [
            jnp.concatenate(lows[j][::-1] + [blocks[j]] + highs[j], axis=dims[j])
            for j in range(len(blocks))
        ]
    return blocks


def inside_mask(block_shape, width):
    parts = []
    for k, axis in enumerate(AXES):
        n = block_shape[k]
        total = n * lax.axis_size(axis)
        coord = lax.axis_index(axis) * n - width + jnp.arange(n + 2 * width)
        parts.append((coord >= 0) & (coord < total))
    return parts[0][:, None, None] & parts[1][None, :, None] & parts[2][None, None, :]


def harmonic(left, right):
    return 2.0 * left * right / (left + right)


def neighbours(padded):
    return (
        padded[2:, 1:-1, 1:-1],
        padded[:-2, 1:-1, 1:-1],
        padded[1:-1, 2:, 1:-1],
        padded[1:-1, :-2, 1:-1],
        padded[1:-1, 1:-1, 2:],
        padded[1:-1, 1:-1, :-2],
    )


def face_set_zero_outside(cond):
    padded = jnp.pad(cond, 1)
    faces = tuple(harmonic(cond, jnp.where(other > 0.0, other, cond)) for other in neighbours(padded))
    diag = faces[0] + faces[1] + faces[2] + faces[3] + faces[4] + faces[5]
    return faces, diag


def operate(field, faces, diag, scale):
    near = neighbours(jnp.pad(field, 1))
    total = faces[0] * near[0] + faces[1] * near[1] + faces[2] * near[2]
    total = total + faces[3] * near[3] + faces[4] * near[4] + faces[5] * near[5]
    return scale * (diag * field - total)


def smooth(right, start, faces, diag, scale, mask=None, operate=operate):
    def keep(value):
        return value if mask is None else jnp.where(mask, value, 0.0)

    theta = 0.5 * (HIGH + LOW)
    delta = 0.5 * (HIGH - LOW)
    sigma = theta / delta
    rho = 1.0 / sigma
    inverse = 1.0 / (scale * diag)
    if start is None:
        resid = right
        step_dir = inverse * resid / theta
        field = keep(step_dir)
    else:
        resid = right - operate(start, faces, diag, scale)
        step_dir = inverse * resid / theta
        field = keep(start + step_dir)
    for turn in range(DEGREE - 1):
        rho_new = 1.0 / (2.0 * sigma - rho)
        resid = right - operate(field, faces, diag, scale)
        step_dir = rho_new * rho * step_dir + 2.0 * rho_new / delta * inverse * resid
        field = keep(field + step_dir)
        rho = rho_new
    return field


def restrict(field):
    field = field[0::2] + field[1::2]
    field = field[:, 0::2] + field[:, 1::2]
    field = field[:, :, 0::2] + field[:, :, 1::2]
    return field / 8.0


def prolong(field):
    return jnp.repeat(jnp.repeat(jnp.repeat(field, 2, 0), 2, 1), 2, 2)


def centre(field, width):
    return field[width:-width, width:-width, width:-width]


def face_set_global(cond):
    padded = jnp.pad(cond, 1, mode="edge")
    faces = tuple(harmonic(cond, other) for other in neighbours(padded))
    diag = faces[0] + faces[1] + faces[2] + faces[3] + faces[4] + faces[5]
    return faces, diag


def neighbours_dilated(padded):
    return (
        padded[2:, 1:-1, 2:-2],
        padded[:-2, 1:-1, 2:-2],
        padded[1:-1, 2:, 2:-2],
        padded[1:-1, :-2, 2:-2],
        padded[1:-1, 1:-1, 4:],
        padded[1:-1, 1:-1, :-4],
    )


def face_set_dilated(cond):
    padded = jnp.concatenate([cond[:, :, :2], cond, cond[:, :, -2:]], axis=2)
    padded = jnp.pad(padded, ((1, 1), (1, 1), (0, 0)), mode="edge")
    faces = tuple(harmonic(cond, other) for other in neighbours_dilated(padded))
    diag = faces[0] + faces[1] + faces[2] + faces[3] + faces[4] + faces[5]
    return faces, diag


def operate_dilated(field, faces, diag, scale):
    near = neighbours_dilated(jnp.pad(field, ((1, 1), (1, 1), (2, 2))))
    total = faces[0] * near[0] + faces[1] * near[1] + faces[2] * near[2]
    total = total + faces[3] * near[3] + faces[4] * near[4] + faces[5] * near[5]
    return scale * (diag * field - total)


def restrict_dilated(field):
    field = field[0::2] + field[1::2]
    field = field[:, 0::2] + field[:, 1::2]
    later = jnp.concatenate([field[:, :, 1:], jnp.zeros_like(field[:, :, :1])], axis=2)
    return (field + later) / 8.0


def prolong_dilated(field):
    earlier = jnp.concatenate([jnp.zeros_like(field[:, :, :1]), field[:, :, :-1]], axis=2)
    odd = (jnp.arange(field.shape[2]) % 2 == 1)[None, None, :]
    field = jnp.where(odd, earlier, field)
    return jnp.repeat(jnp.repeat(field, 2, 0), 2, 1)


def cycle_global(right, cond, scale):
    faces, diag = face_set_global(cond)
    field = smooth(right, None, faces, diag, scale)
    resid = right - operate(field, faces, diag, scale)
    right3, cond3 = restrict_dilated(resid), restrict_dilated(cond)
    faces3, diag3 = face_set_dilated(cond3)
    scale3 = scale * 0.25
    error = smooth(right3, None, faces3, diag3, scale3, operate=operate_dilated)
    error = smooth(right3, error, faces3, diag3, scale3, operate=operate_dilated)
    field = field + prolong_dilated(error)
    return smooth(right, field, faces, diag, scale)


def gather_axis(block, axis, dim, descending=False):
    count = lax.axis_size(axis)
    if count & (count - 1):
        return lax.all_gather(block, axis, axis=dim, tiled=True)
    index = lax.axis_index(axis)
    steps = []
    step = 1
    while step < count:
        steps.append(step)
        step *= 2
    if descending:
        steps = steps[::-1]
    size = block.shape[dim]
    for step in steps:
        theirs = lax.ppermute(block, axis, [(i, i ^ step) for i in range(count)])
        upper = (index // step) % 2 == 1
        low = jnp.where(upper, theirs, block)
        high = jnp.where(upper, block, theirs)
        block = jnp.concatenate([low, high], axis=dim)
    if descending and len(steps) > 1:
        bits = len(steps)
        shape = block.shape
        split = shape[:dim] + (2,) * bits + (size,) + shape[dim + 1:]
        order = (
            list(range(dim))
            + [dim + bits - 1 - b for b in range(bits)]
            + list(range(dim + bits, len(split)))
        )
        block = block.reshape(split).transpose(order).reshape(shape)
    return block


def gather_global(block):
    block = gather_axis(block, "gz", 3)
    block = gather_axis(block, "gy", 2)
    return gather_axis(block, "gx", 1, descending=True)


def local(heat_source, material, conductivity):
    cond0 = jnp.zeros(heat_source.shape, jnp.float32)
    for which in range(MATERIALS):
        cond0 = cond0 + jnp.where(material == which, conductivity[which], jnp.float32(0.0))
    cond1 = restrict(cond0)
    cond2 = restrict(cond1)
    block0, block1 = heat_source.shape, cond1.shape

    ext0, cond1e = exchange([jnp.stack([cond0, heat_source]), cond1], [HALO0, HALO1])
    cond0e, right0e = ext0[0], ext0[1]

    mask0 = inside_mask(block0, HALO0)
    faces0, diag0 = face_set_zero_outside(cond0e)
    field0 = smooth(right0e, None, faces0, diag0, 1.0, mask0)
    resid0 = centre(right0e - operate(field0, faces0, diag0, 1.0), HALO0)

    faces1, diag1 = face_set_zero_outside(cond1e)
    mask1 = inside_mask(block1, HALO1)
    (right1e,) = exchange([restrict(resid0)], [HALO1])
    field1 = smooth(right1e, None, faces1, diag1, 0.25, mask1)
    resid1 = centre(right1e - operate(field1, faces1, diag1, 0.25), HALO1)

    whole = gather_global(jnp.stack([cond2, restrict(resid1)]))
    error2 = cycle_global(whole[1], whole[0], 0.0625)

    reach = HALO1 // 2
    padded2 = jnp.pad(error2, reach)
    block2 = cond2.shape
    starts = [lax.axis_index(axis) * n for axis, n in zip(AXES, block2)]
    sizes = [n + 2 * reach for n in block2]
    error2e = lax.dynamic_slice(padded2, starts, sizes)
    field1 = jnp.where(mask1, field1 + prolong(error2e), 0.0)
    field1 = smooth(right1e, field1, faces1, diag1, 0.25, mask1)

    cut = HALO1 - HALO0 // 2
    error1e = field1[cut:-cut, cut:-cut, cut:-cut]
    field0 = jnp.where(mask0, field0 + prolong(error1e), 0.0)
    field0 = smooth(right0e, field0, faces0, diag0, 1.0, mask0)
    return centre(field0, HALO0)


def solution(mesh):
    in_specs = (P("gx", "gy", "gz"), P("gx", "gy", "gz"), P())
    out_specs = P("gx", "gy", "gz")
    return jax.shard_map(local, mesh=mesh, in_specs=in_specs, out_specs=out_specs, check_vma=False)
```

```python
import jax
import jax.numpy as jnp
from jax import lax
from jax.sharding import PartitionSpec as P

DEGREE = 3
LEVELS = 3
MATERIALS = 3

LOW = 0.3
HIGH = 2.0

AXES = ("gx", "gy", "gz")
HALO0 = 6
HALO1 = 8


def exchange(blocks, widths):
    blocks = list(blocks)
    for k, axis in enumerate(AXES):
        count = lax.axis_size(axis)
        dims = [b.ndim - 3 + k for b in blocks]
        sizes = [b.shape[d] for b, d in zip(blocks, dims)]
        reach = [-(-w // n) for w, n in zip(widths, sizes)]
        lows = [[] for _ in blocks]
        highs = [[] for _ in blocks]
        for shift in range(1, max(reach) + 1):
            users = [j for j in range(len(blocks)) if reach[j] >= shift]
            takes = {j: min(sizes[j], widths[j] - (shift - 1) * sizes[j]) for j in users}
            for side in (0, 1):
                slabs = []
                for j in users:
                    n, t = sizes[j], takes[j]
                    start = n - t if side == 0 else 0
                    slabs.append(lax.slice_in_dim(blocks[j], start, start + t, axis=dims[j]))
                if shift >= count:
                    got = [jnp.zeros_like(s) for s in slabs]
                else:
                    if side == 0:
                        pairs = [(i, i + shift) for i in range(count - shift)]
                    else:
                        pairs = [(i + shift, i) for i in range(count - shift)]
                    flat = jnp.concatenate([s.reshape(-1) for s in slabs])
                    flat = lax.ppermute(flat, axis, pairs)
                    got, at = [], 0
                    for s in slabs:
                        got.append(flat[at:at + s.size].reshape(s.shape))
                        at += s.size
                for j, g in zip(users, got):
                    (lows if side == 0 else highs)[j].append(g)
        blocks = [
            jnp.concatenate(lows[j][::-1] + [blocks[j]] + highs[j], axis=dims[j])
            for j in range(len(blocks))
        ]
    return blocks


def inside_mask(block_shape, width):
    parts = []
    for k, axis in enumerate(AXES):
        n = block_shape[k]
        total = n * lax.axis_size(axis)
        coord = lax.axis_index(axis) * n - width + jnp.arange(n + 2 * width)
        parts.append((coord >= 0) & (coord < total))
    return parts[0][:, None, None] & parts[1][None, :, None] & parts[2][None, None, :]


def harmonic(left, right):
    return 2.0 * left * right / (left + right)


def neighbours(padded):
    return (
        padded[2:, 1:-1, 1:-1],
        padded[:-2, 1:-1, 1:-1],
        padded[1:-1, 2:, 1:-1],
        padded[1:-1, :-2, 1:-1],
        padded[1:-1, 1:-1, 2:],
        padded[1:-1, 1:-1, :-2],
    )


def face_set_zero_outside(cond):
    padded = jnp.pad(cond, 1)
    faces = tuple(harmonic(cond, jnp.where(other > 0.0, other, cond)) for other in neighbours(padded))
    diag = faces[0] + faces[1] + faces[2] + faces[3] + faces[4] + faces[5]
    return faces, diag


def operate(field, faces, diag, scale):
    near = neighbours(jnp.pad(field, 1))
    total = faces[0] * near[0] + faces[1] * near[1] + faces[2] * near[2]
    total = total + faces[3] * near[3] + faces[4] * near[4] + faces[5] * near[5]
    return scale * (diag * field - total)


def smooth(right, start, faces, diag, scale, mask=None, operate=operate):
    def keep(value):
        return value if mask is None else jnp.where(mask, value, 0.0)

    theta = 0.5 * (HIGH + LOW)
    delta = 0.5 * (HIGH - LOW)
    sigma = theta / delta
    rho = 1.0 / sigma
    inverse = 1.0 / (scale * diag)
    if start is None:
        resid = right
        step_dir = inverse * resid / theta
        field = keep(step_dir)
    else:
        resid = right - operate(start, faces, diag, scale)
        step_dir = inverse * resid / theta
        field = keep(start + step_dir)
    for turn in range(DEGREE - 1):
        rho_new = 1.0 / (2.0 * sigma - rho)
        resid = right - operate(field, faces, diag, scale)
        step_dir = rho_new * rho * step_dir + 2.0 * rho_new / delta * inverse * resid
        field = keep(field + step_dir)
        rho = rho_new
    return field


def restrict(field):
    field = field[0::2] + field[1::2]
    field = field[:, 0::2] + field[:, 1::2]
    field = field[:, :, 0::2] + field[:, :, 1::2]
    return field / 8.0


def prolong(field):
    return jnp.repeat(jnp.repeat(jnp.repeat(field, 2, 0), 2, 1), 2, 2)


def centre(field, width):
    return field[width:-width, width:-width, width:-width]


def face_set_global(cond):
    padded = jnp.pad(cond, 1, mode="edge")
    faces = tuple(harmonic(cond, other) for other in neighbours(padded))
    diag = faces[0] + faces[1] + faces[2] + faces[3] + faces[4] + faces[5]
    return faces, diag


def neighbours_dilated(padded):
    return (
        padded[2:, 1:-1, 2:-2],
        padded[:-2, 1:-1, 2:-2],
        padded[1:-1, 2:, 2:-2],
        padded[1:-1, :-2, 2:-2],
        padded[1:-1, 1:-1, 4:],
        padded[1:-1, 1:-1, :-4],
    )


def face_set_dilated(cond):
    padded = jnp.concatenate([cond[:, :, :2], cond, cond[:, :, -2:]], axis=2)
    padded = jnp.pad(padded, ((1, 1), (1, 1), (0, 0)), mode="edge")
    faces = tuple(harmonic(cond, other) for other in neighbours_dilated(padded))
    diag = faces[0] + faces[1] + faces[2] + faces[3] + faces[4] + faces[5]
    return faces, diag


def operate_dilated(field, faces, diag, scale):
    near = neighbours_dilated(jnp.pad(field, ((1, 1), (1, 1), (2, 2))))
    total = faces[0] * near[0] + faces[1] * near[1] + faces[2] * near[2]
    total = total + faces[3] * near[3] + faces[4] * near[4] + faces[5] * near[5]
    return scale * (diag * field - total)


def restrict_dilated(field):
    field = field[0::2] + field[1::2]
    field = field[:, 0::2] + field[:, 1::2]
    later = jnp.concatenate([field[:, :, 1:], jnp.zeros_like(field[:, :, :1])], axis=2)
    return (field + later) / 8.0


def prolong_dilated(field):
    earlier = jnp.concatenate([jnp.zeros_like(field[:, :, :1]), field[:, :, :-1]], axis=2)
    odd = (jnp.arange(field.shape[2]) % 2 == 1)[None, None, :]
    field = jnp.where(odd, earlier, field)
    return jnp.repeat(jnp.repeat(field, 2, 0), 2, 1)


def cycle_global(right, cond, scale):
    faces, diag = face_set_global(cond)
    field = smooth(right, None, faces, diag, scale)
    resid = right - operate(field, faces, diag, scale)
    right3, cond3 = restrict_dilated(resid), restrict_dilated(cond)
    faces3, diag3 = face_set_dilated(cond3)
    scale3 = scale * 0.25
    error = smooth(right3, None, faces3, diag3, scale3, operate=operate_dilated)
    error = smooth(right3, error, faces3, diag3, scale3, operate=operate_dilated)
    field = field + prolong_dilated(error)
    return smooth(right, field, faces, diag, scale)


def gather_axis(block, axis, dim, descending=False):
    count = lax.axis_size(axis)
    if count & (count - 1):
        return lax.all_gather(block, axis, axis=dim, tiled=True)
    index = lax.axis_index(axis)
    steps = []
    step = 1
    while step < count:
        steps.append(step)
        step *= 2
    if descending:
        steps = steps[::-1]
    size = block.shape[dim]
    for step in steps:
        theirs = lax.ppermute(block, axis, [(i, i ^ step) for i in range(count)])
        upper = (index // step) % 2 == 1
        low = jnp.where(upper, theirs, block)
        high = jnp.where(upper, block, theirs)
        block = jnp.concatenate([low, high], axis=dim)
    if descending and len(steps) > 1:
        bits = len(steps)
        shape = block.shape
        split = shape[:dim] + (2,) * bits + (size,) + shape[dim + 1:]
        order = (
            list(range(dim))
            + [dim + bits - 1 - b for b in range(bits)]
            + list(range(dim + bits, len(split)))
        )
        block = block.reshape(split).transpose(order).reshape(shape)
    return block


def gather_global(block):
    block = gather_axis(block, "gz", 3)
    block = gather_axis(block, "gy", 2)
    return gather_axis(block, "gx", 1, descending=True)


def local(heat_source, material, conductivity):
    cond0 = jnp.zeros(heat_source.shape, jnp.float32)
    for which in range(MATERIALS):
        cond0 = cond0 + jnp.where(material == which, conductivity[which], jnp.float32(0.0))
    cond1 = restrict(cond0)
    cond2 = restrict(cond1)
    block0, block1 = heat_source.shape, cond1.shape

    ext0, cond1e = exchange([jnp.stack([cond0, heat_source]), cond1], [HALO0, HALO1])
    cond0e, right0e = ext0[0], ext0[1]

    mask0 = inside_mask(block0, HALO0)
    faces0, diag0 = face_set_zero_outside(cond0e)
    field0 = smooth(right0e, None, faces0, diag0, 1.0, mask0)
    resid0 = centre(right0e - operate(field0, faces0, diag0, 1.0), HALO0)

    faces1, diag1 = face_set_zero_outside(cond1e)
    mask1 = inside_mask(block1, HALO1)
    (right1e,) = exchange([restrict(resid0)], [HALO1 - 1])
    right1e = jnp.pad(right1e, 1)
    field1 = smooth(right1e, None, faces1, diag1, 0.25, mask1)
    resid1 = centre(right1e - operate(field1, faces1, diag1, 0.25), HALO1)

    whole = gather_global(jnp.stack([cond2, restrict(resid1)]))
    error2 = cycle_global(whole[1], whole[0], 0.0625)

    reach = HALO1 // 2
    padded2 = jnp.pad(error2, reach)
    block2 = cond2.shape
    starts = [lax.axis_index(axis) * n for axis, n in zip(AXES, block2)]
    sizes = [n + 2 * reach for n in block2]
    error2e = lax.dynamic_slice(padded2, starts, sizes)
    field1 = jnp.where(mask1, field1 + prolong(error2e), 0.0)
    field1 = smooth(right1e, field1, faces1, diag1, 0.25, mask1)

    cut = HALO1 - HALO0 // 2
    error1e = field1[cut:-cut, cut:-cut, cut:-cut]
    field0 = jnp.where(mask0, field0 + prolong(error1e), 0.0)
    field0 = smooth(right0e, field0, faces0, diag0, 1.0, mask0)
    return centre(field0, HALO0)


def solution(mesh):
    in_specs = (P("gx", "gy", "gz"), P("gx", "gy", "gz"), P())
    out_specs = P("gx", "gy", "gz")
    return jax.shard_map(local, mesh=mesh, in_specs=in_specs, out_specs=out_specs, check_vma=False)
```

```python
import jax
import jax.numpy as jnp
from jax import lax
from jax.sharding import PartitionSpec as P

DEGREE = 3
LEVELS = 3
MATERIALS = 3

LOW = 0.3
HIGH = 2.0

AXES = ("gx", "gy", "gz")
HALO0 = 6
HALO1 = 8


def exchange(blocks, widths):
    blocks = list(blocks)
    for k, axis in enumerate(AXES):
        count = lax.axis_size(axis)
        dims = [b.ndim - 3 + k for b in blocks]
        sizes = [b.shape[d] for b, d in zip(blocks, dims)]
        reach = [-(-w // n) for w, n in zip(widths, sizes)]
        lows = [[] for _ in blocks]
        highs = [[] for _ in blocks]
        for shift in range(1, max(reach) + 1):
            users = [j for j in range(len(blocks)) if reach[j] >= shift]
            takes = {j: min(sizes[j], widths[j] - (shift - 1) * sizes[j]) for j in users}
            for side in (0, 1):
                slabs = []
                for j in users:
                    n, t = sizes[j], takes[j]
                    start = n - t if side == 0 else 0
                    slabs.append(lax.slice_in_dim(blocks[j], start, start + t, axis=dims[j]))
                if shift >= count:
                    got = [jnp.zeros_like(s) for s in slabs]
                else:
                    if side == 0:
                        pairs = [(i, i + shift) for i in range(count - shift)]
                    else:
                        pairs = [(i + shift, i) for i in range(count - shift)]
                    flat = jnp.concatenate([s.reshape(-1) for s in slabs])
                    flat = lax.ppermute(flat, axis, pairs)
                    got, at = [], 0
                    for s in slabs:
                        got.append(flat[at:at + s.size].reshape(s.shape))
                        at += s.size
                for j, g in zip(users, got):
                    (lows if side == 0 else highs)[j].append(g)
        blocks = [
            jnp.concatenate(lows[j][::-1] + [blocks[j]] + highs[j], axis=dims[j])
            for j in range(len(blocks))
        ]
    return blocks


def inside_mask(block_shape, width):
    parts = []
    for k, axis in enumerate(AXES):
        n = block_shape[k]
        total = n * lax.axis_size(axis)
        coord = lax.axis_index(axis) * n - width + jnp.arange(n + 2 * width)
        parts.append((coord >= 0) & (coord < total))
    return parts[0][:, None, None] & parts[1][None, :, None] & parts[2][None, None, :]


def harmonic(left, right):
    return 2.0 * left * right / (left + right)


def neighbours(padded):
    return (
        padded[2:, 1:-1, 1:-1],
        padded[:-2, 1:-1, 1:-1],
        padded[1:-1, 2:, 1:-1],
        padded[1:-1, :-2, 1:-1],
        padded[1:-1, 1:-1, 2:],
        padded[1:-1, 1:-1, :-2],
    )


def face_set_zero_outside(cond):
    padded = jnp.pad(cond, 1)
    faces = tuple(harmonic(cond, jnp.where(other > 0.0, other, cond)) for other in neighbours(padded))
    diag = faces[0] + faces[1] + faces[2] + faces[3] + faces[4] + faces[5]
    return faces, diag


def operate(field, faces, diag, scale):
    near = neighbours(jnp.pad(field, 1))
    total = faces[0] * near[0] + faces[1] * near[1] + faces[2] * near[2]
    total = total + faces[3] * near[3] + faces[4] * near[4] + faces[5] * near[5]
    return scale * (diag * field - total)


def smooth(right, start, faces, diag, scale, mask=None, operate=operate):
    def keep(value):
        return value if mask is None else jnp.where(mask, value, 0.0)

    theta = 0.5 * (HIGH + LOW)
    delta = 0.5 * (HIGH - LOW)
    sigma = theta / delta
    rho = 1.0 / sigma
    inverse = 1.0 / (scale * diag)
    if start is None:
        resid = right
        step_dir = inverse * resid / theta
        field = keep(step_dir)
    else:
        resid = right - operate(start, faces, diag, scale)
        step_dir = inverse * resid / theta
        field = keep(start + step_dir)
    for turn in range(DEGREE - 1):
        rho_new = 1.0 / (2.0 * sigma - rho)
        resid = right - operate(field, faces, diag, scale)
        step_dir = rho_new * rho * step_dir + 2.0 * rho_new / delta * inverse * resid
        field = keep(field + step_dir)
        rho = rho_new
    return field


def restrict(field):
    field = field[0::2] + field[1::2]
    field = field[:, 0::2] + field[:, 1::2]
    field = field[:, :, 0::2] + field[:, :, 1::2]
    return field / 8.0


def prolong(field):
    return jnp.repeat(jnp.repeat(jnp.repeat(field, 2, 0), 2, 1), 2, 2)


def centre(field, width):
    return field[width:-width, width:-width, width:-width]


def face_set_global(cond):
    padded = jnp.pad(cond, 1, mode="edge")
    faces = tuple(harmonic(cond, other) for other in neighbours(padded))
    diag = faces[0] + faces[1] + faces[2] + faces[3] + faces[4] + faces[5]
    return faces, diag


def neighbours_dilated(padded):
    return (
        padded[2:, 1:-1, 2:-2],
        padded[:-2, 1:-1, 2:-2],
        padded[1:-1, 2:, 2:-2],
        padded[1:-1, :-2, 2:-2],
        padded[1:-1, 1:-1, 4:],
        padded[1:-1, 1:-1, :-4],
    )


def face_set_dilated(cond):
    padded = jnp.concatenate([cond[:, :, :2], cond, cond[:, :, -2:]], axis=2)
    padded = jnp.pad(padded, ((1, 1), (1, 1), (0, 0)), mode="edge")
    faces = tuple(harmonic(cond, other) for other in neighbours_dilated(padded))
    diag = faces[0] + faces[1] + faces[2] + faces[3] + faces[4] + faces[5]
    return faces, diag


def operate_dilated(field, faces, diag, scale):
    near = neighbours_dilated(jnp.pad(field, ((1, 1), (1, 1), (2, 2))))
    total = faces[0] * near[0] + faces[1] * near[1] + faces[2] * near[2]
    total = total + faces[3] * near[3] + faces[4] * near[4] + faces[5] * near[5]
    return scale * (diag * field - total)


def restrict_dilated(field):
    field = field[0::2] + field[1::2]
    field = field[:, 0::2] + field[:, 1::2]
    later = jnp.concatenate([field[:, :, 1:], jnp.zeros_like(field[:, :, :1])], axis=2)
    return (field + later) / 8.0


def prolong_dilated(field):
    earlier = jnp.concatenate([jnp.zeros_like(field[:, :, :1]), field[:, :, :-1]], axis=2)
    odd = (jnp.arange(field.shape[2]) % 2 == 1)[None, None, :]
    field = jnp.where(odd, earlier, field)
    return jnp.repeat(jnp.repeat(field, 2, 0), 2, 1)


def cycle_global(right, cond, scale):
    faces, diag = face_set_global(cond)
    field = smooth(right, None, faces, diag, scale)
    resid = right - operate(field, faces, diag, scale)
    right3, cond3 = restrict_dilated(resid), restrict_dilated(cond)
    faces3, diag3 = face_set_dilated(cond3)
    scale3 = scale * 0.25
    error = smooth(right3, None, faces3, diag3, scale3, operate=operate_dilated)
    error = smooth(right3, error, faces3, diag3, scale3, operate=operate_dilated)
    field = field + prolong_dilated(error)
    return smooth(right, field, faces, diag, scale)


def gather_axis(block, axis, dim, descending=False):
    count = lax.axis_size(axis)
    if count & (count - 1):
        return lax.all_gather(block, axis, axis=dim, tiled=True)
    index = lax.axis_index(axis)
    steps = []
    step = 1
    while step < count:
        steps.append(step)
        step *= 2
    if descending:
        steps = steps[::-1]
    size = block.shape[dim]
    for step in steps:
        theirs = lax.ppermute(block, axis, [(i, i ^ step) for i in range(count)])
        upper = (index // step) % 2 == 1
        low = jnp.where(upper, theirs, block)
        high = jnp.where(upper, block, theirs)
        block = jnp.concatenate([low, high], axis=dim)
    if descending and len(steps) > 1:
        bits = len(steps)
        shape = block.shape
        split = shape[:dim] + (2,) * bits + (size,) + shape[dim + 1:]
        order = (
            list(range(dim))
            + [dim + bits - 1 - b for b in range(bits)]
            + list(range(dim + bits, len(split)))
        )
        block = block.reshape(split).transpose(order).reshape(shape)
    return block


def gather_global(block):
    block = gather_axis(block, "gz", 3)
    block = gather_axis(block, "gy", 2)
    return gather_axis(block, "gx", 1, descending=True)


def local(heat_source, material, conductivity):
    cond0 = jnp.zeros(heat_source.shape, jnp.float32)
    for which in range(MATERIALS):
        cond0 = cond0 + jnp.where(material == which, conductivity[which], jnp.float32(0.0))
    cond1 = restrict(cond0)
    cond2 = restrict(cond1)
    block0, block1 = heat_source.shape, cond1.shape

    cond0e, right0e, cond1e = exchange([cond0, heat_source, cond1], [HALO0, HALO0 - 1, HALO1])
    right0e = jnp.pad(right0e, 1)

    mask0 = inside_mask(block0, HALO0)
    faces0, diag0 = face_set_zero_outside(cond0e)
    field0 = smooth(right0e, None, faces0, diag0, 1.0, mask0)
    resid0 = centre(right0e - operate(field0, faces0, diag0, 1.0), HALO0)

    faces1, diag1 = face_set_zero_outside(cond1e)
    mask1 = inside_mask(block1, HALO1)
    (right1e,) = exchange([restrict(resid0)], [HALO1 - 1])
    right1e = jnp.pad(right1e, 1)
    field1 = smooth(right1e, None, faces1, diag1, 0.25, mask1)
    resid1 = centre(right1e - operate(field1, faces1, diag1, 0.25), HALO1)

    whole = gather_global(jnp.stack([cond2, restrict(resid1)]))
    error2 = cycle_global(whole[1], whole[0], 0.0625)

    reach = HALO1 // 2
    padded2 = jnp.pad(error2, reach)
    block2 = cond2.shape
    starts = [lax.axis_index(axis) * n for axis, n in zip(AXES, block2)]
    sizes = [n + 2 * reach for n in block2]
    error2e = lax.dynamic_slice(padded2, starts, sizes)
    field1 = jnp.where(mask1, field1 + prolong(error2e), 0.0)
    field1 = smooth(right1e, field1, faces1, diag1, 0.25, mask1)

    cut = HALO1 - HALO0 // 2
    error1e = field1[cut:-cut, cut:-cut, cut:-cut]
    field0 = jnp.where(mask0, field0 + prolong(error1e), 0.0)
    field0 = smooth(right0e, field0, faces0, diag0, 1.0, mask0)
    return centre(field0, HALO0)


def solution(mesh):
    in_specs = (P("gx", "gy", "gz"), P("gx", "gy", "gz"), P())
    out_specs = P("gx", "gy", "gz")
    return jax.shard_map(local, mesh=mesh, in_specs=in_specs, out_specs=out_specs, check_vma=False)
```
